128 devices in a mesh: row: 4 (over x), col: 32 (over z, y, core).
Axes of the slice: x: 4, y: 4, z: 4, core: 2. Of those that a mesh axis runs over, the one named last changes fastest.
Arguments:
- child_factors: bfloat16 [2, 2048, 8192], P(None, 'col', 'row'), may hold values from -0.0625 to 0.0625
- child_tiles: int32 [2, 16], replicated, may hold values from 0 to 63, as said below
- root_diag: float32 [8192], P('col'), may hold values from 0.5 to 4
Outputs:
- front_out: float32 [8192, 8192], P('row', 'col')
The draws below stay inside these ranges and needn't reach their ends.
Inputs may be any that keep to these rules, and one draw needn't show every extreme that they name: `child_tiles`: each row lists 2048 / 128 distinct root tiles in increasing order; the first child's list holds tile 0 and the second child's holds the last tile. For every r below 4, exactly 2048 / (128 * 4) tiles t of each row have ((t * 128) // 256) % 4 == r.
All inputs are finite; a program needn't handle non-finite values.
Results may differ from the reference program's by a relative error of at most 0.0003.
Values may be sent and summed in bfloat16 or wider, within the bound.
No kernel may reach another device: no remote copies, remote signals or barrier semaphores. Data moves between devices by JAX's collectives and lax.ppermute only.
A program may use at most 128 MiB of HBM per device.

```python
import math
import jax
import jax.numpy as jnp
from jax import lax

NF = 8192
NU = 2048
RC = 8192
TILE = 128
NPAN = 1
N_ROW = 4
N_COL = 32


def pick_tiles(key, forced):
    tile_total = NF // TILE
    per_owner = NU // (TILE * N_ROW)
    block_size = NF // N_COL
    index = jnp.arange(tile_total, dtype=jnp.int32)
    owner = index * TILE // block_size % N_ROW
    ranking = jax.random.permutation(key, tile_total).astype(jnp.int32)
    ranking = jnp.where(index == forced, -1, ranking)
    score = owner * (tile_total + 2) + ranking + 1
    ordered = jnp.argsort(score).astype(jnp.int32)
    chosen = ordered.reshape(N_ROW, tile_total // N_ROW)[:, :per_owner].reshape(-1)
    return jnp.sort(chosen).astype(jnp.int32)


def draw_child_tiles(key, part):
    first_child = pick_tiles(jax.random.fold_in(key, 11), 0)
    second = pick_tiles(jax.random.fold_in(key, 12), NF // TILE - 1)
    return jnp.stack([first_child, second]).astype(jnp.int32)


def level_of(stream_key, shape, cuts, low, high):
    gain, own = 1.0, jax.random.fold_in(stream_key, 6)
    for axis_at, shards_of in cuts:
        heights = jnp.exp(jax.random.uniform(jax.random.fold_in(own, axis_at), (shards_of,), jnp.float32, low / len(cuts), high / len(cuts)))
        gain = gain * jnp.repeat(heights, shape[axis_at] // shards_of).reshape([-1 if axis == axis_at else 1 for axis in range(len(shape))])
    return gain


def centred(stream_key, dims, scale, most, cuts=(), held_as=jnp.bfloat16):
    gain = level_of(stream_key, dims, cuts, -0.22, 0.18) if cuts else 1.0
    values = jax.random.normal(stream_key, dims, jnp.float32) * scale * gain
    return jnp.minimum(jnp.maximum(values, -most), most).astype(held_as)


def setup_inputs(seed: int = 0) -> dict:
    key_list = jax.random.split(jax.random.key(seed), 4)
    return {
        "child_factors": centred(key_list[0], (2, NU, RC), RC ** -0.5, 0.0625, ((1, 32), (2, 4))),
        "child_tiles": draw_child_tiles(jax.random.fold_in(key_list[3], 71), 0),
        "root_diag": jnp.clip(jnp.exp(math.log(4.0) - 2.0794415 * jax.random.uniform(key_list[2], (NF,), jnp.float32) ** level_of(key_list[2], (NF,), ((0, 32),), -0.2, 0.2)), 0.5, 4.0),
    }


def reference(child_factors, child_tiles, root_diag):
    order_total = root_diag.shape[0]
    block_size = order_total // N_COL
    loc_rows = order_total // N_ROW
    front = jnp.diag(root_diag).astype(jnp.float32)
    offsets = jnp.arange(TILE, dtype=jnp.int32)
    for child in range(2):
        gram_block = jnp.dot(child_factors[child].astype(jnp.float32), child_factors[child].T.astype(jnp.float32), preferred_element_type=jnp.float32)
        parent_rows = (child_tiles[child][:, None] * TILE + offsets[None, :]).reshape(-1).astype(jnp.int32)
        front = front.at[parent_rows[:, None], parent_rows[None, :]].add(gram_block)
    leading = NPAN * block_size
    lead_factor = jnp.tril(jnp.linalg.cholesky(front[:leading, :leading]))
    below_factor = lax.linalg.triangular_solve(lead_factor, front[leading:, :leading], left_side=False, lower=True, transpose_a=True)
    schur_block = front[leading:, leading:] - jnp.dot(below_factor, below_factor.T, precision=lax.Precision.HIGHEST)
    result = jnp.zeros_like(front)
    result = result.at[:leading, :leading].set(lead_factor)
    result = result.at[leading:, :leading].set(below_factor)
    result = result.at[leading:, leading:].set(schur_block)
    stored = jnp.arange(order_total, dtype=jnp.int32)
    global_row = (stored // loc_rows + stored % loc_rows // block_size * N_ROW) * block_size + stored % block_size
    return result[global_row.astype(jnp.int32)]
```

```python
import jax
import jax.numpy as jnp
from jax import lax
from jax.sharding import PartitionSpec as P

TILE = 128
NPAN = 1


def pick_tiles(tiles4, index):
    return jnp.take_along_axis(tiles4, index[:, :, None, None], axis=1)


def shards(child_factors, child_tiles, root_diag):
    highest = lax.Precision.HIGHEST
    row_count = lax.axis_size("row")
    block_size = root_diag.shape[0]
    col_count = lax.axis_size("col")
    order_total = block_size * col_count
    loc_rows = order_total // row_count
    row_index = lax.axis_index("row")
    col_index = lax.axis_index("col")
    n_child = child_tiles.shape[0]
    tiles_child = child_tiles.shape[1]
    per_group = tiles_child // row_count
    tiles_block = block_size // TILE
    loc_tiles = loc_rows // TILE

    gathered = lax.all_gather(child_factors, "col", axis=1, tiled=True)
    k_loc = gathered.shape[2]
    tiles4 = gathered.reshape(n_child, tiles_child, TILE, k_loc)
    full_diag = lax.all_gather(root_diag, "col", axis=0, tiled=True)

    owner = (child_tiles * TILE // block_size) % row_count
    position = jnp.arange(tiles_child, dtype=jnp.int32)
    key = owner * tiles_child + position[None, :]
    rank = jnp.sum(key[:, None, :] < key[:, :, None], axis=2).astype(jnp.int32)
    order = jnp.sum(
        jnp.where(rank[:, :, None] == position[None, None, :], position[None, :, None], 0),
        axis=1,
    ).astype(jnp.int32)
    grouped = pick_tiles(tiles4, order)

    own_tiles = col_index * tiles_block + jnp.arange(tiles_block, dtype=jnp.int32)
    pivot_tiles = jnp.arange(NPAN * tiles_block, dtype=jnp.int32)
    wanted = jnp.concatenate([own_tiles, pivot_tiles])
    match = child_tiles[:, :, None] == wanted[None, None, :]
    where_at = jnp.sum(jnp.where(match, position[None, :, None], 0), axis=1).astype(jnp.int32)
    present = jnp.any(match, axis=1)
    col_rows = pick_tiles(tiles4, where_at)
    col_rows = jnp.where(present[:, :, None, None], col_rows, jnp.zeros_like(col_rows))
    n_cols = wanted.shape[0] * TILE
    col_rows = col_rows.reshape(n_child, n_cols, k_loc)
    pivot_rows = col_rows[:, tiles_block * TILE :]

    grouped = grouped.reshape(n_child, row_count, per_group * TILE, k_loc)
    main = jnp.einsum(
        "cgnk,cmk->gcnm", grouped, col_rows, preferred_element_type=jnp.float32
    )
    extra = jnp.einsum(
        "cnk,cmk->cnm", pivot_rows, col_rows, preferred_element_type=jnp.float32
    )
    extra = jnp.broadcast_to(extra[None], (row_count,) + extra.shape)
    packed = jnp.concatenate([main, extra], axis=2)
    chunk_rows = packed.shape[2]
    reduced = lax.psum_scatter(
        packed.reshape(row_count * n_child * chunk_rows, n_cols),
        "row",
        scatter_dimension=0,
        tiled=True,
    ).reshape(n_child, chunk_rows, n_cols)
    mine = reduced[:, : per_group * TILE]
    pivot_part = jnp.sum(reduced[:, per_group * TILE :], axis=0)

    own_w = tiles_block * TILE
    lead_rows = NPAN * block_size
    pivot_diag = full_diag[:lead_rows]
    front00 = pivot_part[:, own_w:] + jnp.diag(pivot_diag)
    lead = jnp.tril(jnp.linalg.cholesky(front00))
    inv_t = lax.linalg.triangular_solve(
        lead, jnp.eye(lead_rows, dtype=jnp.float32), left_side=False, lower=True, transpose_a=True
    )
    cols_panel = jnp.where(col_index == 0, front00, pivot_part[:, :own_w]).T

    my_tiles = lax.dynamic_slice_in_dim(order, row_index * per_group, per_group, axis=1)
    my_root = jnp.take_along_axis(child_tiles, my_tiles, axis=1)
    my_local = (my_root * TILE // block_size) // row_count * tiles_block + my_root % tiles_block
    loc_index = jnp.arange(loc_tiles, dtype=jnp.int32)
    hit = my_local[:, None, :] == loc_index[None, :, None]
    src = jnp.sum(jnp.where(hit, jnp.arange(per_group, dtype=jnp.int32)[None, None, :], 0), axis=2)
    got = jnp.any(hit, axis=2)
    mine4 = mine.reshape(n_child, per_group, TILE, n_cols)
    placed = pick_tiles(mine4, src.astype(jnp.int32))
    placed = jnp.where(got[:, :, None, None], placed, jnp.zeros_like(placed))
    front_loc = jnp.sum(placed, axis=0).reshape(loc_rows, n_cols)

    local_rows = jnp.arange(loc_rows, dtype=jnp.int32)
    row_block = row_index + local_rows // block_size * row_count
    glob_rows = row_block * block_size + local_rows % block_size
    glob_cols = col_index * block_size + jnp.arange(block_size, dtype=jnp.int32)
    diag_own = jnp.where(glob_rows[:, None] == glob_cols[None, :], root_diag[None, :], 0.0)
    diag_pivot = jnp.where(
        glob_rows[:, None] == jnp.arange(lead_rows, dtype=jnp.int32)[None, :],
        pivot_diag[None, :],
        0.0,
    )
    front_own = front_loc[:, :own_w] + diag_own
    front_pivot = front_loc[:, own_w:] + diag_pivot

    below_rows = jnp.dot(front_pivot, inv_t, precision=highest)
    below_cols = jnp.dot(cols_panel, inv_t, precision=highest)
    schur = front_own - jnp.dot(below_rows, below_cols.T, precision=highest)

    in_lead = (row_block < NPAN)[:, None]
    lead_tiled = jnp.tile(lead, (loc_rows // lead_rows, 1))
    first_col = jnp.where(in_lead, lead_tiled, below_rows)
    rest = jnp.where(in_lead, 0.0, schur)
    return jnp.where(col_index < NPAN, first_col, rest)


def solution(mesh):
    placed = (P(None, "col", "row"), P(), P("col"))
    return jax.shard_map(
        shards, mesh=mesh, in_specs=placed, out_specs=P("row", "col"), check_vma=False
    )
```

```python
import jax
import jax.numpy as jnp
from jax import lax
from jax.sharding import PartitionSpec as P

TILE = 128
NPAN = 1


def pick_tiles(tiles4, index):
    return jnp.take_along_axis(tiles4, index[:, :, None, None], axis=1)


def shards(child_factors, child_tiles, root_diag):
    highest = lax.Precision.HIGHEST
    row_count = lax.axis_size("row")
    block_size = root_diag.shape[0]
    col_count = lax.axis_size("col")
    order_total = block_size * col_count
    loc_rows = order_total // row_count
    row_index = lax.axis_index("row")
    col_index = lax.axis_index("col")
    n_child = child_tiles.shape[0]
    tiles_child = child_tiles.shape[1]
    per_group = tiles_child // row_count
    tiles_block = block_size // TILE
    loc_tiles = loc_rows // TILE

    gathered = lax.all_gather(child_factors, "col", axis=1, tiled=True)
    k_loc = gathered.shape[2]
    tiles4 = gathered.reshape(n_child, tiles_child, TILE, k_loc)
    full_diag = lax.all_gather(root_diag, "col", axis=0, tiled=True)

    owner = (child_tiles * TILE // block_size) % row_count
    position = jnp.arange(tiles_child, dtype=jnp.int32)
    key = owner * tiles_child + position[None, :]
    rank = jnp.sum(key[:, None, :] < key[:, :, None], axis=2).astype(jnp.int32)
    order = jnp.sum(
        jnp.where(rank[:, :, None] == position[None, None, :], position[None, :, None], 0),
        axis=1,
    ).astype(jnp.int32)
    grouped = pick_tiles(tiles4, order)

    own_tiles = col_index * tiles_block + jnp.arange(tiles_block, dtype=jnp.int32)
    pivot_tiles = jnp.arange(NPAN * tiles_block, dtype=jnp.int32)
    wanted = jnp.concatenate([own_tiles, pivot_tiles])
    match = child_tiles[:, :, None] == wanted[None, None, :]
    where_at = jnp.sum(jnp.where(match, position[None, :, None], 0), axis=1).astype(jnp.int32)
    present = jnp.any(match, axis=1)
    col_rows = pick_tiles(tiles4, where_at)
    col_rows = jnp.where(present[:, :, None, None], col_rows, jnp.zeros_like(col_rows))
    n_cols = wanted.shape[0] * TILE
    col_rows = col_rows.reshape(n_child, n_cols, k_loc)
    pivot_rows = col_rows[:, tiles_block * TILE :]

    extra = jnp.einsum(
        "cnk,cmk->nm", pivot_rows, col_rows, preferred_element_type=jnp.float32
    )
    pivot_part = lax.psum(extra, "row")

    grouped = grouped.reshape(n_child, row_count, per_group * TILE, k_loc)
    main = jnp.einsum(
        "cgnk,cmk->gcnm", grouped, col_rows, preferred_element_type=jnp.float32
    )
    mine = lax.psum_scatter(
        main.reshape(row_count * n_child * per_group * TILE, n_cols),
        "row",
        scatter_dimension=0,
        tiled=True,
    ).reshape(n_child, per_group * TILE, n_cols)

    own_w = tiles_block * TILE
    lead_rows = NPAN * block_size
    pivot_diag = full_diag[:lead_rows]
    front00 = pivot_part[:, own_w:] + jnp.diag(pivot_diag)
    lead = jnp.tril(jnp.linalg.cholesky(front00))
    inv_t = lax.linalg.triangular_solve(
        lead, jnp.eye(lead_rows, dtype=jnp.float32), left_side=False, lower=True, transpose_a=True
    )
    cols_panel = jnp.where(col_index == 0, front00, pivot_part[:, :own_w]).T

    my_tiles = lax.dynamic_slice_in_dim(order, row_index * per_group, per_group, axis=1)
    my_root = jnp.take_along_axis(child_tiles, my_tiles, axis=1)
    my_local = (my_root * TILE // block_size) // row_count * tiles_block + my_root % tiles_block
    loc_index = jnp.arange(loc_tiles, dtype=jnp.int32)
    hit = my_local[:, None, :] == loc_index[None, :, None]
    src = jnp.sum(jnp.where(hit, jnp.arange(per_group, dtype=jnp.int32)[None, None, :], 0), axis=2)
    got = jnp.any(hit, axis=2)
    mine4 = mine.reshape(n_child, per_group, TILE, n_cols)
    placed = pick_tiles(mine4, src.astype(jnp.int32))
    placed = jnp.where(got[:, :, None, None], placed, jnp.zeros_like(placed))
    front_loc = jnp.sum(placed, axis=0).reshape(loc_rows, n_cols)

    local_rows = jnp.arange(loc_rows, dtype=jnp.int32)
    row_block = row_index + local_rows // block_size * row_count
    glob_rows = row_block * block_size + local_rows % block_size
    glob_cols = col_index * block_size + jnp.arange(block_size, dtype=jnp.int32)
    diag_own = jnp.where(glob_rows[:, None] == glob_cols[None, :], root_diag[None, :], 0.0)
    front_own = front_loc[:, :own_w] + diag_own
    front_pivot = front_loc[:, own_w:]

    below_rows = jnp.dot(front_pivot, inv_t, precision=highest)
    below_cols = jnp.dot(cols_panel, inv_t, precision=highest)
    schur = front_own - jnp.dot(below_rows, below_cols.T, precision=highest)

    in_lead = (row_block < NPAN)[:, None]
    lead_tiled = jnp.tile(lead, (loc_rows // lead_rows, 1))
    first_col = jnp.where(in_lead, lead_tiled, below_rows)
    rest = jnp.where(in_lead, 0.0, schur)
    return jnp.where(col_index < NPAN, first_col, rest)


def solution(mesh):
    placed = (P(None, "col", "row"), P(), P("col"))
    return jax.shard_map(
        shards, mesh=mesh, in_specs=placed, out_specs=P("row", "col"), check_vma=False
    )
```

```python
import jax
import jax.numpy as jnp
from jax import lax
from jax.sharding import PartitionSpec as P

TILE = 128
NPAN = 1


def pick_tiles(tiles4, index):
    return jnp.take_along_axis(tiles4, index[:, :, None, None], axis=1)


def shards(child_factors, child_tiles, root_diag):
    highest = lax.Precision.HIGHEST
    row_count = lax.axis_size("row")
    block_size = root_diag.shape[0]
    col_count = lax.axis_size("col")
    order_total = block_size * col_count
    loc_rows = order_total // row_count
    row_index = lax.axis_index("row")
    col_index = lax.axis_index("col")
    n_child = child_tiles.shape[0]
    tiles_child = child_tiles.shape[1]
    per_group = tiles_child // row_count
    tiles_block = block_size // TILE
    loc_tiles = loc_rows // TILE

    diag_hi = lax.reduce_precision(root_diag, exponent_bits=8, mantissa_bits=7)
    diag_rest = root_diag - diag_hi
    diag_mid = lax.reduce_precision(diag_rest, exponent_bits=8, mantissa_bits=7)
    diag_lo = diag_rest - diag_mid
    diag_parts = jnp.stack([diag_hi, diag_mid, diag_lo]).astype(jnp.bfloat16).reshape(-1, TILE)
    rows_here = child_factors.shape[1]
    diag_block = jnp.zeros((rows_here, TILE), jnp.bfloat16)
    diag_block = lax.dynamic_update_slice(diag_block, diag_parts, (0, 0))

    owner = (child_tiles * TILE // block_size) % row_count
    position = jnp.arange(tiles_child, dtype=jnp.int32)
    key = owner * tiles_child + position[None, :]
    rank = jnp.sum(key[:, None, :] < key[:, :, None], axis=2).astype(jnp.int32)
    order = jnp.sum(
        jnp.where(rank[:, :, None] == position[None, None, :], position[None, :, None], 0),
        axis=1,
    ).astype(jnp.int32)
    own_tiles = col_index * tiles_block + jnp.arange(tiles_block, dtype=jnp.int32)
    pivot_tiles = jnp.arange(NPAN * tiles_block, dtype=jnp.int32)
    wanted = jnp.concatenate([own_tiles, pivot_tiles])
    match = child_tiles[:, :, None] == wanted[None, None, :]
    where_at = jnp.sum(jnp.where(match, position[None, :, None], 0), axis=1).astype(jnp.int32)
    present = jnp.any(match, axis=1)
    n_cols = wanted.shape[0] * TILE

    mine_parts = []
    extra = None
    carry = None
    for child in range(n_child):
        factors = child_factors[child]
        k_loc = factors.shape[1]
        last = child == n_child - 1
        if carry is not None:
            factors = factors + carry
        if last:
            factors = jnp.concatenate([factors, diag_block], axis=1)
        gathered = lax.all_gather(factors, "col", axis=0, tiled=True)
        if last:
            diag_all = gathered[:, k_loc:].reshape(col_count, rows_here, TILE)
            diag_all = diag_all[:, : diag_parts.shape[0]].reshape(col_count, 3, block_size)
            diag_all = diag_all.astype(jnp.float32)
            full_diag = ((diag_all[:, 0] + diag_all[:, 1]) + diag_all[:, 2]).reshape(-1)
            gathered = gathered[:, :k_loc]
        tiles3 = gathered.reshape(tiles_child, TILE, k_loc)
        carry = (gathered[:1] * 0).astype(factors.dtype)
        col_rows = jnp.take(tiles3, where_at[child], axis=0)
        col_rows = jnp.where(present[child][:, None, None], col_rows, jnp.zeros_like(col_rows))
        col_rows = col_rows.reshape(n_cols, k_loc)
        pivot_rows = col_rows[tiles_block * TILE :]
        term = jnp.einsum("nk,mk->nm", pivot_rows, col_rows, preferred_element_type=jnp.float32)
        extra = term if extra is None else extra + term
        if last:
            pivot_part = extra
            for shift in range(1, row_count):
                pairs = [(i, (i + shift) % row_count) for i in range(row_count)]
                pivot_part = pivot_part + lax.ppermute(extra, "row", pairs)
            tiles3 = tiles3 + (pivot_part[:1, :1] * 0).astype(tiles3.dtype)[None]
        grouped = jnp.take(tiles3, order[child], axis=0)
        grouped = grouped.reshape(row_count, per_group * TILE, k_loc)
        main = jnp.einsum("gnk,mk->gnm", grouped, col_rows, preferred_element_type=jnp.float32)
        mine_parts.append(
            lax.psum_scatter(
                main.reshape(row_count * per_group * TILE, n_cols),
                "row",
                scatter_dimension=0,
                tiled=True,
            )
        )
    mine = jnp.stack(mine_parts)

    own_w = tiles_block * TILE
    lead_rows = NPAN * block_size
    pivot_diag = full_diag[:lead_rows]
    front00 = pivot_part[:, own_w:] + jnp.diag(pivot_diag)
    lead = jnp.tril(jnp.linalg.cholesky(front00))
    inv_t = lax.linalg.triangular_solve(
        lead, jnp.eye(lead_rows, dtype=jnp.float32), left_side=False, lower=True, transpose_a=True
    )
    cols_panel = jnp.where(col_index == 0, front00, pivot_part[:, :own_w]).T

    my_tiles = lax.dynamic_slice_in_dim(order, row_index * per_group, per_group, axis=1)
    my_root = jnp.take_along_axis(child_tiles, my_tiles, axis=1)
    my_local = (my_root * TILE // block_size) // row_count * tiles_block + my_root % tiles_block
    loc_index = jnp.arange(loc_tiles, dtype=jnp.int32)
    hit = my_local[:, None, :] == loc_index[None, :, None]
    src = jnp.sum(jnp.where(hit, jnp.arange(per_group, dtype=jnp.int32)[None, None, :], 0), axis=2)
    got = jnp.any(hit, axis=2)
    mine4 = mine.reshape(n_child, per_group, TILE, n_cols)
    placed = pick_tiles(mine4, src.astype(jnp.int32))
    placed = jnp.where(got[:, :, None, None], placed, jnp.zeros_like(placed))
    front_loc = jnp.sum(placed, axis=0).reshape(loc_rows, n_cols)

    local_rows = jnp.arange(loc_rows, dtype=jnp.int32)
    row_block = row_index + local_rows // block_size * row_count
    glob_rows = row_block * block_size + local_rows % block_size
    glob_cols = col_index * block_size + jnp.arange(block_size, dtype=jnp.int32)
    diag_own = jnp.where(glob_rows[:, None] == glob_cols[None, :], root_diag[None, :], 0.0)
    front_own = front_loc[:, :own_w] + diag_own
    front_pivot = front_loc[:, own_w:]

    below_rows = jnp.dot(front_pivot, inv_t, precision=highest)
    below_cols = jnp.dot(cols_panel, inv_t, precision=highest)
    schur = front_own - jnp.dot(below_rows, below_cols.T, precision=highest)

    in_lead = (row_block < NPAN)[:, None]
    lead_tiled = jnp.tile(lead, (loc_rows // lead_rows, 1))
    first_col = jnp.where(in_lead, lead_tiled, below_rows)
    rest = jnp.where(in_lead, 0.0, schur)
    return jnp.where(col_index < NPAN, first_col, rest)


def solution(mesh):
    placed = (P(None, "col", "row"), P(), P("col"))
    return jax.shard_map(
        shards, mesh=mesh, in_specs=placed, out_specs=P("row", "col"), check_vma=False
    )
```

```python
import jax
import jax.numpy as jnp
from jax import lax
from jax.sharding import PartitionSpec as P

TILE = 128
NPAN = 1


def pick_tiles(tiles4, index):
    return jnp.take_along_axis(tiles4, index[:, :, None, None], axis=1)


def shards(child_factors, child_tiles, root_diag):
    highest = lax.Precision.HIGHEST
    row_count = lax.axis_size("row")
    block_size = root_diag.shape[0]
    col_count = lax.axis_size("col")
    order_total = block_size * col_count
    loc_rows = order_total // row_count
    row_index = lax.axis_index("row")
    col_index = lax.axis_index("col")
    n_child = child_tiles.shape[0]
    tiles_child = child_tiles.shape[1]
    per_group = tiles_child // row_count
    tiles_block = block_size // TILE
    loc_tiles = loc_rows // TILE

    gathered = lax.all_gather(child_factors, "col", axis=1, tiled=True)
    k_loc = gathered.shape[2]
    tiles4 = gathered.reshape(n_child, tiles_child, TILE, k_loc)
    full_diag = lax.all_gather(root_diag, "col", axis=0, tiled=True)
    diag_edge = (full_diag[0] * 0).astype(jnp.int32)

    owner = (child_tiles * TILE // block_size) % row_count
    position = jnp.arange(tiles_child, dtype=jnp.int32)
    key = owner * tiles_child + position[None, :]
    rank = jnp.sum(key[:, None, :] < key[:, :, None], axis=2).astype(jnp.int32)
    order = jnp.sum(
        jnp.where(rank[:, :, None] == position[None, None, :], position[None, :, None], 0),
        axis=1,
    ).astype(jnp.int32)
    grouped = pick_tiles(tiles4, order)

    own_tiles = col_index * tiles_block + jnp.arange(tiles_block, dtype=jnp.int32)
    pivot_tiles = jnp.arange(NPAN * tiles_block, dtype=jnp.int32)
    wanted = jnp.concatenate([own_tiles, pivot_tiles])
    match = child_tiles[:, :, None] == wanted[None, None, :]
    where_at = jnp.sum(jnp.where(match, position[None, :, None], 0), axis=1).astype(jnp.int32)
    where_at = where_at + diag_edge
    present = jnp.any(match, axis=1)
    col_rows = pick_tiles(tiles4, where_at)
    col_rows = jnp.where(present[:, :, None, None], col_rows, jnp.zeros_like(col_rows))
    n_cols = wanted.shape[0] * TILE
    col_rows = col_rows.reshape(n_child, n_cols, k_loc)
    pivot_rows = col_rows[:, tiles_block * TILE :]

    extra = jnp.einsum(
        "cnk,cmk->nm", pivot_rows, col_rows, preferred_element_type=jnp.float32
    )
    pivot_part = extra
    for shift in range(1, row_count):
        pairs = [(i, (i + shift) % row_count) for i in range(row_count)]
        pivot_part = pivot_part + lax.ppermute(extra, "row", pairs)
    grouped = grouped + (extra[:1, :1] * 0).astype(grouped.dtype)[None, None]

    grouped = grouped.reshape(n_child, row_count, per_group * TILE, k_loc)
    main = jnp.einsum(
        "cgnk,cmk->gcnm", grouped, col_rows, preferred_element_type=jnp.float32
    )
    main = main + (pivot_part[:1, :1] * 0)[None, None]
    mine = lax.psum_scatter(
        main.reshape(row_count * n_child * per_group * TILE, n_cols),
        "row",
        scatter_dimension=0,
        tiled=True,
    ).reshape(n_child, per_group * TILE, n_cols)

    own_w = tiles_block * TILE
    lead_rows = NPAN * block_size
    pivot_diag = full_diag[:lead_rows]
    front00 = pivot_part[:, own_w:] + jnp.diag(pivot_diag)
    lead = jnp.tril(jnp.linalg.cholesky(front00))
    inv_t = lax.linalg.triangular_solve(
        lead, jnp.eye(lead_rows, dtype=jnp.float32), left_side=False, lower=True, transpose_a=True
    )
    cols_panel = jnp.where(col_index == 0, front00, pivot_part[:, :own_w]).T

    my_tiles = lax.dynamic_slice_in_dim(order, row_index * per_group, per_group, axis=1)
    my_root = jnp.take_along_axis(child_tiles, my_tiles, axis=1)
    my_local = (my_root * TILE // block_size) // row_count * tiles_block + my_root % tiles_block
    loc_index = jnp.arange(loc_tiles, dtype=jnp.int32)
    hit = my_local[:, None, :] == loc_index[None, :, None]
    src = jnp.sum(jnp.where(hit, jnp.arange(per_group, dtype=jnp.int32)[None, None, :], 0), axis=2)
    got = jnp.any(hit, axis=2)
    mine4 = mine.reshape(n_child, per_group, TILE, n_cols)
    placed = pick_tiles(mine4, src.astype(jnp.int32))
    placed = jnp.where(got[:, :, None, None], placed, jnp.zeros_like(placed))
    front_loc = jnp.sum(placed, axis=0).reshape(loc_rows, n_cols)

    local_rows = jnp.arange(loc_rows, dtype=jnp.int32)
    row_block = row_index + local_rows // block_size * row_count
    glob_rows = row_block * block_size + local_rows % block_size
    glob_cols = col_index * block_size + jnp.arange(block_size, dtype=jnp.int32)
    diag_own = jnp.where(glob_rows[:, None] == glob_cols[None, :], root_diag[None, :], 0.0)
    front_own = front_loc[:, :own_w] + diag_own
    front_pivot = front_loc[:, own_w:]

    below_rows = jnp.dot(front_pivot, inv_t, precision=highest)
    below_cols = jnp.dot(cols_panel, inv_t, precision=highest)
    schur = front_own - jnp.dot(below_rows, below_cols.T, precision=highest)

    in_lead = (row_block < NPAN)[:, None]
    lead_tiled = jnp.tile(lead, (loc_rows // lead_rows, 1))
    first_col = jnp.where(in_lead, lead_tiled, below_rows)
    rest = jnp.where(in_lead, 0.0, schur)
    return jnp.where(col_index < NPAN, first_col, rest)


def solution(mesh):
    placed = (P(None, "col", "row"), P(), P("col"))
    return jax.shard_map(
        shards, mesh=mesh, in_specs=placed, out_specs=P("row", "col"), check_vma=False
    )
```

```python
import jax
import jax.numpy as jnp
from jax import lax
from jax.sharding import PartitionSpec as P

TILE = 128
NPAN = 1


def pick_tiles(tiles4, index):
    return jnp.take_along_axis(tiles4, index[:, :, None, None], axis=1)


def shards(child_factors, child_tiles, root_diag):
    highest = lax.Precision.HIGHEST
    row_count = lax.axis_size("row")
    block_size = root_diag.shape[0]
    col_count = lax.axis_size("col")
    order_total = block_size * col_count
    loc_rows = order_total // row_count
    row_index = lax.axis_index("row")
    col_index = lax.axis_index("col")
    n_child = child_tiles.shape[0]
    tiles_child = child_tiles.shape[1]
    per_group = tiles_child // row_count
    tiles_block = block_size // TILE
    loc_tiles = loc_rows // TILE

    gathered = lax.all_gather(child_factors, "col", axis=1, tiled=True)
    k_loc = gathered.shape[2]
    tiles4 = gathered.reshape(n_child, tiles_child, TILE, k_loc)
    full_diag = lax.all_gather(root_diag, "col", axis=0, tiled=True)
    diag_edge = (full_diag[0] * 0).astype(jnp.int32)

    owner = (child_tiles * TILE // block_size) % row_count
    position = jnp.arange(tiles_child, dtype=jnp.int32)
    key = owner * tiles_child + position[None, :]
    rank = jnp.sum(key[:, None, :] < key[:, :, None], axis=2).astype(jnp.int32)
    order = jnp.sum(
        jnp.where(rank[:, :, None] == position[None, None, :], position[None, :, None], 0),
        axis=1,
    ).astype(jnp.int32)

    own_tiles = col_index * tiles_block + jnp.arange(tiles_block, dtype=jnp.int32)
    pivot_tiles = jnp.arange(NPAN * tiles_block, dtype=jnp.int32)
    wanted = jnp.concatenate([own_tiles, pivot_tiles])
    match = child_tiles[:, :, None] == wanted[None, None, :]
    where_at = jnp.sum(jnp.where(match, position[None, :, None], 0), axis=1).astype(jnp.int32)
    where_at = where_at + diag_edge
    present = jnp.any(match, axis=1)
    col_rows = pick_tiles(tiles4, where_at)
    col_rows = jnp.where(present[:, :, None, None], col_rows, jnp.zeros_like(col_rows))
    n_cols = wanted.shape[0] * TILE
    col_rows = col_rows.reshape(n_child, n_cols, k_loc)
    pivot_rows = col_rows[:, tiles_block * TILE :]

    extra = jnp.einsum(
        "cnk,cmk->nm", pivot_rows, col_rows, preferred_element_type=jnp.float32
    )
    pivot_part = extra
    for shift in range(1, row_count):
        pairs = [(i, (i + shift) % row_count) for i in range(row_count)]
        pivot_part = pivot_part + lax.ppermute(extra, "row", pairs)
    main_rows = col_rows + (extra[:1, :1] * 0).astype(col_rows.dtype)[None]
    main = jnp.einsum(
        "cuk,cmk->cum", gathered, main_rows, preferred_element_type=jnp.float32
    )
    main = main.reshape(n_child * tiles_child, TILE, n_cols)
    child_base = (jnp.arange(n_child, dtype=jnp.int32) * tiles_child)[:, None]
    flat_order = (order + child_base).reshape(n_child, row_count, per_group)
    flat_order = jnp.transpose(flat_order, (1, 0, 2)).reshape(-1)
    flat_order = flat_order + (pivot_part[0, 0] * 0).astype(jnp.int32)
    main = jnp.take(main, flat_order, axis=0)
    mine = lax.psum_scatter(
        main.reshape(row_count * n_child * per_group * TILE, n_cols),
        "row",
        scatter_dimension=0,
        tiled=True,
    ).reshape(n_child, per_group * TILE, n_cols)

    own_w = tiles_block * TILE
    lead_rows = NPAN * block_size
    pivot_diag = full_diag[:lead_rows]
    front00 = pivot_part[:, own_w:] + jnp.diag(pivot_diag)
    lead = jnp.tril(jnp.linalg.cholesky(front00))
    inv_t = lax.linalg.triangular_solve(
        lead, jnp.eye(lead_rows, dtype=jnp.float32), left_side=False, lower=True, transpose_a=True
    )
    cols_panel = jnp.where(col_index == 0, front00, pivot_part[:, :own_w]).T

    my_tiles = lax.dynamic_slice_in_dim(order, row_index * per_group, per_group, axis=1)
    my_root = jnp.take_along_axis(child_tiles, my_tiles, axis=1)
    my_local = (my_root * TILE // block_size) // row_count * tiles_block + my_root % tiles_block
    loc_index = jnp.arange(loc_tiles, dtype=jnp.int32)
    hit = my_local[:, None, :] == loc_index[None, :, None]
    src = jnp.sum(jnp.where(hit, jnp.arange(per_group, dtype=jnp.int32)[None, None, :], 0), axis=2)
    got = jnp.any(hit, axis=2)
    mine4 = mine.reshape(n_child, per_group, TILE, n_cols)
    placed = pick_tiles(mine4, src.astype(jnp.int32))
    placed = jnp.where(got[:, :, None, None], placed, jnp.zeros_like(placed))
    front_loc = jnp.sum(placed, axis=0).reshape(loc_rows, n_cols)

    local_rows = jnp.arange(loc_rows, dtype=jnp.int32)
    row_block = row_index + local_rows // block_size * row_count
    glob_rows = row_block * block_size + local_rows % block_size
    glob_cols = col_index * block_size + jnp.arange(block_size, dtype=jnp.int32)
    diag_own = jnp.where(glob_rows[:, None] == glob_cols[None, :], root_diag[None, :], 0.0)
    front_own = front_loc[:, :own_w] + diag_own
    front_pivot = front_loc[:, own_w:]

    below_rows = jnp.dot(front_pivot, inv_t, precision=highest)
    below_cols = jnp.dot(cols_panel, inv_t, precision=highest)
    schur = front_own - jnp.dot(below_rows, below_cols.T, precision=highest)

    in_lead = (row_block < NPAN)[:, None]
    lead_tiled = jnp.tile(lead, (loc_rows // lead_rows, 1))
    first_col = jnp.where(in_lead, lead_tiled, below_rows)
    rest = jnp.where(in_lead, 0.0, schur)
    return jnp.where(col_index < NPAN, first_col, rest)


def solution(mesh):
    placed = (P(None, "col", "row"), P(), P("col"))
    return jax.shard_map(
        shards, mesh=mesh, in_specs=placed, out_specs=P("row", "col"), check_vma=False
    )
```

```python
import jax
import jax.numpy as jnp
from jax import lax
from jax.sharding import PartitionSpec as P

TILE = 128
NPAN = 1


def pick_tiles(tiles4, index):
    return jnp.take_along_axis(tiles4, index[:, :, None, None], axis=1, mode="clip")


def shards(child_factors, child_tiles, root_diag):
    highest = lax.Precision.HIGHEST
    row_count = lax.axis_size("row")
    block_size = root_diag.shape[0]
    col_count = lax.axis_size("col")
    order_total = block_size * col_count
    loc_rows = order_total // row_count
    row_index = lax.axis_index("row")
    col_index = lax.axis_index("col")
    n_child = child_tiles.shape[0]
    tiles_child = child_tiles.shape[1]
    per_group = tiles_child // row_count
    tiles_block = block_size // TILE
    loc_tiles = loc_rows // TILE

    gathered = lax.all_gather(child_factors, "col", axis=1, tiled=True)
    k_loc = gathered.shape[2]
    tiles4 = gathered.reshape(n_child, tiles_child, TILE, k_loc)
    full_diag = lax.all_gather(root_diag, "col", axis=0, tiled=True)
    diag_edge = (full_diag[0] * 0).astype(jnp.int32)

    owner = (child_tiles * TILE // block_size) % row_count
    position = jnp.arange(tiles_child, dtype=jnp.int32)
    key = owner * tiles_child + position[None, :]
    rank = jnp.sum(key[:, None, :] < key[:, :, None], axis=2).astype(jnp.int32)
    order = jnp.sum(
        jnp.where(rank[:, :, None] == position[None, None, :], position[None, :, None], 0),
        axis=1,
    ).astype(jnp.int32)

    own_tiles = col_index * tiles_block + jnp.arange(tiles_block, dtype=jnp.int32)
    pivot_tiles = jnp.arange(NPAN * tiles_block, dtype=jnp.int32)
    wanted = jnp.concatenate([own_tiles, pivot_tiles])
    match = child_tiles[:, :, None] == wanted[None, None, :]
    where_at = jnp.sum(jnp.where(match, position[None, :, None], 0), axis=1).astype(jnp.int32)
    where_at = where_at + diag_edge
    present = jnp.any(match, axis=1)
    col_rows = pick_tiles(tiles4, where_at)
    col_rows = jnp.where(present[:, :, None, None], col_rows, jnp.zeros_like(col_rows))
    n_cols = wanted.shape[0] * TILE
    col_rows = col_rows.reshape(n_child, n_cols, k_loc)
    pivot_rows = col_rows[:, tiles_block * TILE :]

    extra = jnp.einsum(
        "cnk,cmk->nm", pivot_rows, col_rows, preferred_element_type=jnp.float32
    )
    pivot_part = extra
    for shift in range(1, row_count):
        pairs = [(i, (i + shift) % row_count) for i in range(row_count)]
        pivot_part = pivot_part + lax.ppermute(extra, "row", pairs)
    main_rows = col_rows + (extra[:1, :1] * 0).astype(col_rows.dtype)[None]
    main = jnp.einsum(
        "cutk,cmk->cutm", tiles4, main_rows, preferred_element_type=jnp.float32
    )
    main = main.reshape(n_child * tiles_child, TILE, n_cols)
    child_base = (jnp.arange(n_child, dtype=jnp.int32) * tiles_child)[:, None]
    flat_order = (order + child_base).reshape(n_child, row_count, per_group)
    flat_order = jnp.transpose(flat_order, (1, 0, 2)).reshape(-1)
    flat_order = flat_order + (pivot_part[0, 0] * 0).astype(jnp.int32)
    main = jnp.take(main, flat_order, axis=0, mode="clip")
    mine = lax.psum_scatter(
        main.reshape(row_count * n_child * per_group * TILE, n_cols),
        "row",
        scatter_dimension=0,
        tiled=True,
    ).reshape(n_child, per_group * TILE, n_cols)

    own_w = tiles_block * TILE
    lead_rows = NPAN * block_size
    pivot_diag = full_diag[:lead_rows]
    front00 = pivot_part[:, own_w:] + jnp.diag(pivot_diag)
    lead = jnp.tril(jnp.linalg.cholesky(front00))
    inv_t = lax.linalg.triangular_solve(
        lead, jnp.eye(lead_rows, dtype=jnp.float32), left_side=False, lower=True, transpose_a=True
    )
    cols_panel = jnp.where(col_index == 0, front00, pivot_part[:, :own_w]).T

    my_tiles = lax.dynamic_slice_in_dim(order, row_index * per_group, per_group, axis=1)
    my_root = jnp.take_along_axis(child_tiles, my_tiles, axis=1)
    my_local = (my_root * TILE // block_size) // row_count * tiles_block + my_root % tiles_block
    loc_index = jnp.arange(loc_tiles, dtype=jnp.int32)
    hit = my_local[:, None, :] == loc_index[None, :, None]
    src = jnp.sum(jnp.where(hit, jnp.arange(per_group, dtype=jnp.int32)[None, None, :], 0), axis=2)
    got = jnp.any(hit, axis=2)
    mine4 = mine.reshape(n_child, per_group, TILE, n_cols)
    placed = pick_tiles(mine4, src.astype(jnp.int32))
    placed = jnp.where(got[:, :, None, None], placed, jnp.zeros_like(placed))
    front_loc = jnp.sum(placed, axis=0).reshape(loc_rows, n_cols)

    local_rows = jnp.arange(loc_rows, dtype=jnp.int32)
    row_block = row_index + local_rows // block_size * row_count
    glob_rows = row_block * block_size + local_rows % block_size
    glob_cols = col_index * block_size + jnp.arange(block_size, dtype=jnp.int32)
    diag_own = jnp.where(glob_rows[:, None] == glob_cols[None, :], root_diag[None, :], 0.0)
    front_own = front_loc[:, :own_w] + diag_own
    front_pivot = front_loc[:, own_w:]

    below_rows = jnp.dot(front_pivot, inv_t, precision=highest)
    below_cols = jnp.dot(cols_panel, inv_t, precision=highest)
    schur = front_own - jnp.dot(below_rows, below_cols.T, precision=highest)

    in_lead = (row_block < NPAN)[:, None]
    lead_tiled = jnp.tile(lead, (loc_rows // lead_rows, 1))
    first_col = jnp.where(in_lead, lead_tiled, below_rows)
    rest = jnp.where(in_lead, 0.0, schur)
    return jnp.where(col_index < NPAN, first_col, rest)


def solution(mesh):
    placed = (P(None, "col", "row"), P(), P("col"))
    return jax.shard_map(
        shards, mesh=mesh, in_specs=placed, out_specs=P("row", "col"), check_vma=False
    )
```

```python
import jax
import jax.numpy as jnp
from jax import lax
from jax.sharding import PartitionSpec as P

TILE = 128
NPAN = 1


def pick_tiles(tiles4, index):
    return jnp.take_along_axis(tiles4, index[:, :, None, None], axis=1, mode="clip")


def shards(child_factors, child_tiles, root_diag):
    highest = lax.Precision.HIGHEST
    row_count = lax.axis_size("row")
    block_size = root_diag.shape[0]
    col_count = lax.axis_size("col")
    order_total = block_size * col_count
    loc_rows = order_total // row_count
    row_index = lax.axis_index("row")
    col_index = lax.axis_index("col")
    n_child = child_tiles.shape[0]
    tiles_child = child_tiles.shape[1]
    per_group = tiles_child // row_count
    tiles_block = block_size // TILE
    loc_tiles = loc_rows // TILE

    gathered = lax.all_gather(child_factors, "col", axis=1, tiled=True)
    k_loc = gathered.shape[2]
    tiles4 = gathered.reshape(n_child, tiles_child, TILE, k_loc)
    full_diag = lax.all_gather(root_diag, "col", axis=0, tiled=True)
    diag_edge = (full_diag[0] * 0).astype(jnp.int32)

    owner = (child_tiles * TILE // block_size) % row_count
    position = jnp.arange(tiles_child, dtype=jnp.int32)
    key = owner * tiles_child + position[None, :]
    rank = jnp.sum(key[:, None, :] < key[:, :, None], axis=2).astype(jnp.int32)
    order = jnp.sum(
        jnp.where(rank[:, :, None] == position[None, None, :], position[None, :, None], 0),
        axis=1,
    ).astype(jnp.int32)

    own_tiles = col_index * tiles_block + jnp.arange(tiles_block, dtype=jnp.int32)
    pivot_tiles = jnp.arange(NPAN * tiles_block, dtype=jnp.int32)
    wanted = jnp.concatenate([own_tiles, pivot_tiles])
    match = child_tiles[:, :, None] == wanted[None, None, :]
    where_at = jnp.sum(jnp.where(match, position[None, :, None], 0), axis=1).astype(jnp.int32)
    where_at = where_at + diag_edge
    present = jnp.any(match, axis=1)
    col_rows = jnp.stack(
        [
            jnp.stack(
                [
                    lax.dynamic_index_in_dim(tiles4[child], where_at[child, slot], 0, keepdims=False)
                    for slot in range(where_at.shape[1])
                ]
            )
            for child in range(n_child)
        ]
    )
    col_rows = jnp.where(present[:, :, None, None], col_rows, jnp.zeros_like(col_rows))
    n_cols = wanted.shape[0] * TILE
    col_rows = col_rows.reshape(n_child, n_cols, k_loc)
    pivot_rows = col_rows[:, tiles_block * TILE :]

    extra = jnp.einsum(
        "cnk,cmk->nm", pivot_rows, col_rows, preferred_element_type=jnp.float32
    )
    pivot_part = extra
    for shift in range(1, row_count):
        pairs = [(i, (i + shift) % row_count) for i in range(row_count)]
        pivot_part = pivot_part + lax.ppermute(extra, "row", pairs)
    main_rows = col_rows + (extra[:1, :1] * 0).astype(col_rows.dtype)[None]
    main = jnp.einsum(
        "cutk,cmk->cutm", tiles4, main_rows, preferred_element_type=jnp.float32
    )
    main = main.reshape(n_child * tiles_child, TILE, n_cols)
    child_base = (jnp.arange(n_child, dtype=jnp.int32) * tiles_child)[:, None]
    flat_order = (order + child_base).reshape(n_child, row_count, per_group)
    flat_order = jnp.transpose(flat_order, (1, 0, 2)).reshape(-1)
    flat_order = flat_order + (pivot_part[0, 0] * 0).astype(jnp.int32)
    main = jnp.take(main, flat_order, axis=0, mode="clip")
    mine = lax.psum_scatter(
        main.reshape(row_count * n_child * per_group * TILE, n_cols),
        "row",
        scatter_dimension=0,
        tiled=True,
    ).reshape(n_child, per_group * TILE, n_cols)

    own_w = tiles_block * TILE
    lead_rows = NPAN * block_size
    pivot_diag = full_diag[:lead_rows]
    front00 = pivot_part[:, own_w:] + jnp.diag(pivot_diag)
    lead = jnp.tril(jnp.linalg.cholesky(front00))
    inv_t = lax.linalg.triangular_solve(
        lead, jnp.eye(lead_rows, dtype=jnp.float32), left_side=False, lower=True, transpose_a=True
    )
    cols_panel = jnp.where(col_index == 0, front00, pivot_part[:, :own_w]).T

    my_tiles = lax.dynamic_slice_in_dim(order, row_index * per_group, per_group, axis=1)
    my_root = jnp.take_along_axis(child_tiles, my_tiles, axis=1)
    my_local = (my_root * TILE // block_size) // row_count * tiles_block + my_root % tiles_block
    loc_index = jnp.arange(loc_tiles, dtype=jnp.int32)
    hit = my_local[:, None, :] == loc_index[None, :, None]
    src = jnp.sum(jnp.where(hit, jnp.arange(per_group, dtype=jnp.int32)[None, None, :], 0), axis=2)
    got = jnp.any(hit, axis=2)
    mine4 = mine.reshape(n_child, per_group, TILE, n_cols)
    placed = pick_tiles(mine4, src.astype(jnp.int32))
    placed = jnp.where(got[:, :, None, None], placed, jnp.zeros_like(placed))
    front_loc = jnp.sum(placed, axis=0).reshape(loc_rows, n_cols)

    local_rows = jnp.arange(loc_rows, dtype=jnp.int32)
    row_block = row_index + local_rows // block_size * row_count
    glob_rows = row_block * block_size + local_rows % block_size
    glob_cols = col_index * block_size + jnp.arange(block_size, dtype=jnp.int32)
    diag_own = jnp.where(glob_rows[:, None] == glob_cols[None, :], root_diag[None, :], 0.0)
    front_own = front_loc[:, :own_w] + diag_own
    front_pivot = front_loc[:, own_w:]

    below_rows = jnp.dot(front_pivot, inv_t, precision=highest)
    below_cols = jnp.dot(cols_panel, inv_t, precision=highest)
    schur = front_own - jnp.dot(below_rows, below_cols.T, precision=highest)

    in_lead = (row_block < NPAN)[:, None]
    lead_tiled = jnp.tile(lead, (loc_rows // lead_rows, 1))
    first_col = jnp.where(in_lead, lead_tiled, below_rows)
    rest = jnp.where(in_lead, 0.0, schur)
    return jnp.where(col_index < NPAN, first_col, rest)


def solution(mesh):
    placed = (P(None, "col", "row"), P(), P("col"))
    return jax.shard_map(
        shards, mesh=mesh, in_specs=placed, out_specs=P("row", "col"), check_vma=False
    )
```

```python
import jax
import jax.numpy as jnp
from jax import lax
from jax.sharding import PartitionSpec as P

TILE = 128
NPAN = 1


def pick_tiles(tiles4, index):
    return jnp.take_along_axis(tiles4, index[:, :, None, None], axis=1, mode="clip")


def shards(child_factors, child_tiles, root_diag):
    highest = lax.Precision.HIGHEST
    row_count = lax.axis_size("row")
    block_size = root_diag.shape[0]
    col_count = lax.axis_size("col")
    order_total = block_size * col_count
    loc_rows = order_total // row_count
    row_index = lax.axis_index("row")
    col_index = lax.axis_index("col")
    n_child = child_tiles.shape[0]
    tiles_child = child_tiles.shape[1]
    per_group = tiles_child // row_count
    tiles_block = block_size // TILE
    loc_tiles = loc_rows // TILE

    gathered = lax.all_gather(child_factors, "col", axis=1, tiled=True)
    k_loc = gathered.shape[2]
    tiles4 = gathered.reshape(n_child, tiles_child, TILE, k_loc)
    full_diag = lax.all_gather(root_diag, "col", axis=0, tiled=True)
    diag_edge = (full_diag[0] * 0).astype(jnp.int32)

    owner = (child_tiles * TILE // block_size) % row_count
    position = jnp.arange(tiles_child, dtype=jnp.int32)
    key = owner * tiles_child + position[None, :]
    rank = jnp.sum(key[:, None, :] < key[:, :, None], axis=2).astype(jnp.int32)
    order = jnp.sum(
        jnp.where(rank[:, :, None] == position[None, None, :], position[None, :, None], 0),
        axis=1,
    ).astype(jnp.int32)

    own_tiles = col_index * tiles_block + jnp.arange(tiles_block, dtype=jnp.int32)
    pivot_tiles = jnp.arange(NPAN * tiles_block, dtype=jnp.int32)
    wanted = jnp.concatenate([own_tiles, pivot_tiles])
    match = child_tiles[:, :, None] == wanted[None, None, :]
    where_at = jnp.sum(jnp.where(match, position[None, :, None], 0), axis=1).astype(jnp.int32)
    where_at = where_at + diag_edge
    present = jnp.any(match, axis=1)
    col_rows = jnp.stack(
        [
            jnp.stack(
                [
                    lax.dynamic_index_in_dim(tiles4[child], where_at[child, slot], 0, keepdims=False)
                    for slot in range(where_at.shape[1])
                ]
            )
            for child in range(n_child)
        ]
    )
    col_rows = jnp.where(present[:, :, None, None], col_rows, jnp.zeros_like(col_rows))
    n_cols = wanted.shape[0] * TILE
    col_rows = col_rows.reshape(n_child, n_cols, k_loc)
    pivot_rows = col_rows[:, tiles_block * TILE :]

    extra = jnp.einsum(
        "cnk,cmk->nm", pivot_rows, col_rows, preferred_element_type=jnp.float32
    )
    pivot_part = extra
    for shift in range(1, row_count):
        pairs = [(i, (i + shift) % row_count) for i in range(row_count)]
        pivot_part = pivot_part + lax.ppermute(extra, "row", pairs)
    main_rows = col_rows + (extra[:1, :1] * 0).astype(col_rows.dtype)[None]
    main = jnp.einsum(
        "cutk,cmk->cutm", tiles4, main_rows, preferred_element_type=jnp.float32
    )
    main = main.reshape(n_child * tiles_child, TILE, n_cols)
    child_base = (jnp.arange(n_child, dtype=jnp.int32) * tiles_child)[:, None]
    flat_order = (order + child_base).reshape(n_child, row_count, per_group)
    flat_order = jnp.transpose(flat_order, (1, 0, 2)).reshape(-1)
    flat_order = flat_order + (pivot_part[0, 0] * 0).astype(jnp.int32)
    main = jnp.take(main, flat_order, axis=0, mode="clip")
    mine = lax.psum_scatter(
        main.reshape(row_count * n_child * per_group * TILE, n_cols),
        "row",
        scatter_dimension=0,
        tiled=True,
    ).reshape(n_child, per_group * TILE, n_cols)

    own_w = tiles_block * TILE
    lead_rows = NPAN * block_size
    pivot_diag = full_diag[:lead_rows]
    front00 = pivot_part[:, own_w:] + jnp.diag(pivot_diag)
    lead = jnp.tril(jnp.linalg.cholesky(front00))
    inv_t = lax.linalg.triangular_solve(
        lead, jnp.eye(lead_rows, dtype=jnp.float32), left_side=False, lower=True, transpose_a=True
    )
    cols_panel = jnp.where(col_index == 0, front00, pivot_part[:, :own_w]).T

    my_tiles = lax.dynamic_slice_in_dim(order, row_index * per_group, per_group, axis=1)
    my_root = jnp.take_along_axis(child_tiles, my_tiles, axis=1)
    my_local = (my_root * TILE // block_size) // row_count * tiles_block + my_root % tiles_block
    mine4 = mine.reshape(n_child, per_group, TILE, n_cols)
    front_loc = jnp.zeros((loc_tiles, TILE, n_cols), jnp.float32)
    for child in range(n_child):
        for slot in range(per_group):
            at = my_local[child, slot]
            here = lax.dynamic_index_in_dim(front_loc, at, 0, keepdims=True)
            front_loc = lax.dynamic_update_index_in_dim(
                front_loc, here + mine4[child, slot][None], at, 0
            )
    front_loc = front_loc.reshape(loc_rows, n_cols)

    local_rows = jnp.arange(loc_rows, dtype=jnp.int32)
    row_block = row_index + local_rows // block_size * row_count
    glob_rows = row_block * block_size + local_rows % block_size
    glob_cols = col_index * block_size + jnp.arange(block_size, dtype=jnp.int32)
    diag_own = jnp.where(glob_rows[:, None] == glob_cols[None, :], root_diag[None, :], 0.0)
    front_own = front_loc[:, :own_w] + diag_own
    front_pivot = front_loc[:, own_w:]

    below_rows = jnp.dot(front_pivot, inv_t, precision=highest)
    below_cols = jnp.dot(cols_panel, inv_t, precision=highest)
    schur = front_own - jnp.dot(below_rows, below_cols.T, precision=highest)

    in_lead = (row_block < NPAN)[:, None]
    lead_tiled = jnp.tile(lead, (loc_rows // lead_rows, 1))
    first_col = jnp.where(in_lead, lead_tiled, below_rows)
    rest = jnp.where(in_lead, 0.0, schur)
    return jnp.where(col_index < NPAN, first_col, rest)


def solution(mesh):
    placed = (P(None, "col", "row"), P(), P("col"))
    return jax.shard_map(
        shards, mesh=mesh, in_specs=placed, out_specs=P("row", "col"), check_vma=False
    )
```

```python
import jax
import jax.numpy as jnp
from jax import lax
from jax.sharding import PartitionSpec as P

TILE = 128
NPAN = 1


def pick_tiles(tiles4, index):
    return jnp.take_along_axis(tiles4, index[:, :, None, None], axis=1, mode="clip")


def shards(child_factors, child_tiles, root_diag):
    highest = lax.Precision.HIGHEST
    row_count = lax.axis_size("row")
    block_size = root_diag.shape[0]
    col_count = lax.axis_size("col")
    order_total = block_size * col_count
    loc_rows = order_total // row_count
    row_index = lax.axis_index("row")
    col_index = lax.axis_index("col")
    n_child = child_tiles.shape[0]
    tiles_child = child_tiles.shape[1]
    per_group = tiles_child // row_count
    tiles_block = block_size // TILE
    loc_tiles = loc_rows // TILE

    gathered = lax.all_gather(child_factors, "col", axis=1, tiled=True)
    k_loc = gathered.shape[2]
    tiles4 = gathered.reshape(n_child, tiles_child, TILE, k_loc)
    full_diag = lax.all_gather(root_diag, "col", axis=0, tiled=True)
    diag_edge = (full_diag[0] * 0).astype(jnp.int32)

    owner = (child_tiles * TILE // block_size) % row_count
    position = jnp.arange(tiles_child, dtype=jnp.int32)
    key = owner * tiles_child + position[None, :]
    rank = jnp.sum(key[:, None, :] < key[:, :, None], axis=2).astype(jnp.int32)
    order = jnp.sum(
        jnp.where(rank[:, :, None] == position[None, None, :], position[None, :, None], 0),
        axis=1,
    ).astype(jnp.int32)

    own_tiles = col_index * tiles_block + jnp.arange(tiles_block, dtype=jnp.int32)
    pivot_tiles = jnp.arange(NPAN * tiles_block, dtype=jnp.int32)
    wanted = jnp.concatenate([own_tiles, pivot_tiles])
    match = child_tiles[:, :, None] == wanted[None, None, :]
    where_at = jnp.sum(jnp.where(match, position[None, :, None], 0), axis=1).astype(jnp.int32)
    where_at = where_at + diag_edge
    present = jnp.any(match, axis=1)
    col_rows = jnp.stack(
        [
            jnp.stack(
                [
                    lax.dynamic_index_in_dim(tiles4[child], where_at[child, slot], 0, keepdims=False)
                    for slot in range(where_at.shape[1])
                ]
            )
            for child in range(n_child)
        ]
    )
    col_rows = jnp.where(present[:, :, None, None], col_rows, jnp.zeros_like(col_rows))
    n_cols = wanted.shape[0] * TILE
    col_rows = col_rows.reshape(n_child, n_cols, k_loc)
    pivot_rows = col_rows[:, tiles_block * TILE :]

    extra = jnp.einsum(
        "cnk,cmk->nm", pivot_rows, col_rows, preferred_element_type=jnp.float32
    )
    pivot_part = extra
    for shift in range(1, row_count):
        pairs = [(i, (i + shift) % row_count) for i in range(row_count)]
        pivot_part = pivot_part + lax.ppermute(extra, "row", pairs)
    main_rows = col_rows + (extra[:1, :1] * 0).astype(col_rows.dtype)[None]
    main = jnp.einsum(
        "cutk,cmk->cumt", tiles4, main_rows, preferred_element_type=jnp.float32
    )
    main = main.reshape(n_child * tiles_child, n_cols, TILE)
    child_base = (jnp.arange(n_child, dtype=jnp.int32) * tiles_child)[:, None]
    flat_order = (order + child_base).reshape(n_child, row_count, per_group)
    flat_order = jnp.transpose(flat_order, (1, 0, 2)).reshape(-1)
    flat_order = flat_order + (pivot_part[0, 0] * 0).astype(jnp.int32)
    main = jnp.take(main, flat_order, axis=0, mode="clip")
    mine = lax.psum_scatter(
        main.reshape(row_count * n_child * per_group * n_cols, TILE),
        "row",
        scatter_dimension=0,
        tiled=True,
    ).reshape(n_child, per_group, n_cols, TILE)
    mine = jnp.transpose(mine, (0, 1, 3, 2))

    own_w = tiles_block * TILE
    lead_rows = NPAN * block_size
    pivot_diag = full_diag[:lead_rows]
    front00 = pivot_part[:, own_w:] + jnp.diag(pivot_diag)
    lead = jnp.tril(jnp.linalg.cholesky(front00))
    inv_t = lax.linalg.triangular_solve(
        lead, jnp.eye(lead_rows, dtype=jnp.float32), left_side=False, lower=True, transpose_a=True
    )
    cols_panel = jnp.where(col_index == 0, front00, pivot_part[:, :own_w]).T

    my_tiles = lax.dynamic_slice_in_dim(order, row_index * per_group, per_group, axis=1)
    my_root = jnp.take_along_axis(child_tiles, my_tiles, axis=1)
    my_local = (my_root * TILE // block_size) // row_count * tiles_block + my_root % tiles_block
    mine4 = mine
    front_loc = jnp.zeros((loc_tiles, TILE, n_cols), jnp.float32)
    for child in range(n_child):
        for slot in range(per_group):
            at = my_local[child, slot]
            here = lax.dynamic_index_in_dim(front_loc, at, 0, keepdims=True)
            front_loc = lax.dynamic_update_index_in_dim(
                front_loc, here + mine4[child, slot][None], at, 0
            )
    front_loc = front_loc.reshape(loc_rows, n_cols)

    local_rows = jnp.arange(loc_rows, dtype=jnp.int32)
    row_block = row_index + local_rows // block_size * row_count
    glob_rows = row_block * block_size + local_rows % block_size
    glob_cols = col_index * block_size + jnp.arange(block_size, dtype=jnp.int32)
    diag_own = jnp.where(glob_rows[:, None] == glob_cols[None, :], root_diag[None, :], 0.0)
    front_own = front_loc[:, :own_w] + diag_own
    front_pivot = front_loc[:, own_w:]

    below_rows = jnp.dot(front_pivot, inv_t, precision=highest)
    below_cols = jnp.dot(cols_panel, inv_t, precision=highest)
    schur = front_own - jnp.dot(below_rows, below_cols.T, precision=highest)

    in_lead = (row_block < NPAN)[:, None]
    lead_tiled = jnp.tile(lead, (loc_rows // lead_rows, 1))
    first_col = jnp.where(in_lead, lead_tiled, below_rows)
    rest = jnp.where(in_lead, 0.0, schur)
    return jnp.where(col_index < NPAN, first_col, rest)


def solution(mesh):
    placed = (P(None, "col", "row"), P(), P("col"))
    return jax.shard_map(
        shards, mesh=mesh, in_specs=placed, out_specs=P("row", "col"), check_vma=False
    )
```

```python
import jax
import jax.numpy as jnp
from jax import lax
from jax.sharding import PartitionSpec as P

TILE = 128
NPAN = 1


def pick_tiles(tiles4, index):
    return jnp.take_along_axis(tiles4, index[:, :, None, None], axis=1, mode="clip")


def shards(child_factors, child_tiles, root_diag):
    highest = lax.Precision.HIGHEST
    row_count = lax.axis_size("row")
    block_size = root_diag.shape[0]
    col_count = lax.axis_size("col")
    order_total = block_size * col_count
    loc_rows = order_total // row_count
    row_index = lax.axis_index("row")
    col_index = lax.axis_index("col")
    n_child = child_tiles.shape[0]
    tiles_child = child_tiles.shape[1]
    per_group = tiles_child // row_count
    tiles_block = block_size // TILE
    loc_tiles = loc_rows // TILE

    parity = [[c for c in range(col_count) if c % 2 == p] for p in range(2)]
    half = lax.all_gather(child_factors, "col", axis=1, tiled=True, axis_index_groups=parity)
    other = lax.ppermute(half, "col", [(c, c ^ 1) for c in range(col_count)])
    core = col_index % 2
    even = jnp.where(core == 0, half, other)
    odd = jnp.where(core == 0, other, half)
    n_rows_dev = child_factors.shape[1]
    gathered = jnp.stack(
        [even.reshape(2, -1, n_rows_dev, even.shape[2]), odd.reshape(2, -1, n_rows_dev, odd.shape[2])],
        axis=2,
    ).reshape(2, -1, even.shape[2])
    k_loc = gathered.shape[2]
    tiles4 = gathered.reshape(n_child, tiles_child, TILE, k_loc)
    full_diag = lax.all_gather(root_diag, "col", axis=0, tiled=True)
    diag_edge = (full_diag[0] * 0).astype(jnp.int32)

    owner = (child_tiles * TILE // block_size) % row_count
    position = jnp.arange(tiles_child, dtype=jnp.int32)
    key = owner * tiles_child + position[None, :]
    rank = jnp.sum(key[:, None, :] < key[:, :, None], axis=2).astype(jnp.int32)
    order = jnp.sum(
        jnp.where(rank[:, :, None] == position[None, None, :], position[None, :, None], 0),
        axis=1,
    ).astype(jnp.int32)

    own_tiles = col_index * tiles_block + jnp.arange(tiles_block, dtype=jnp.int32)
    pivot_tiles = jnp.arange(NPAN * tiles_block, dtype=jnp.int32)
    wanted = jnp.concatenate([own_tiles, pivot_tiles])
    match = child_tiles[:, :, None] == wanted[None, None, :]
    where_at = jnp.sum(jnp.where(match, position[None, :, None], 0), axis=1).astype(jnp.int32)
    where_at = where_at + diag_edge
    present = jnp.any(match, axis=1)
    col_rows = jnp.stack(
        [
            jnp.stack(
                [
                    lax.dynamic_index_in_dim(tiles4[child], where_at[child, slot], 0, keepdims=False)
                    for slot in range(where_at.shape[1])
                ]
            )
            for child in range(n_child)
        ]
    )
    col_rows = jnp.where(present[:, :, None, None], col_rows, jnp.zeros_like(col_rows))
    n_cols = wanted.shape[0] * TILE
    col_rows = col_rows.reshape(n_child, n_cols, k_loc)
    pivot_rows = col_rows[:, tiles_block * TILE :]

    extra = jnp.einsum(
        "cnk,cmk->nm", pivot_rows, col_rows, preferred_element_type=jnp.float32
    )
    pivot_part = extra
    for shift in range(1, row_count):
        pairs = [(i, (i + shift) % row_count) for i in range(row_count)]
        pivot_part = pivot_part + lax.ppermute(extra, "row", pairs)
    main_rows = col_rows + (extra[:1, :1] * 0).astype(col_rows.dtype)[None]
    main = jnp.einsum(
        "cutk,cmk->cutm", tiles4, main_rows, preferred_element_type=jnp.float32
    )
    main = main.reshape(n_child * tiles_child, TILE, n_cols)
    child_base = (jnp.arange(n_child, dtype=jnp.int32) * tiles_child)[:, None]
    flat_order = (order + child_base).reshape(n_child, row_count, per_group)
    flat_order = jnp.transpose(flat_order, (1, 0, 2)).reshape(-1)
    flat_order = flat_order + (pivot_part[0, 0] * 0).astype(jnp.int32)
    main = jnp.take(main, flat_order, axis=0, mode="clip")
    mine = lax.psum_scatter(
        main.reshape(row_count * n_child * per_group * TILE, n_cols),
        "row",
        scatter_dimension=0,
        tiled=True,
    ).reshape(n_child, per_group * TILE, n_cols)

    own_w = tiles_block * TILE
    lead_rows = NPAN * block_size
    pivot_diag = full_diag[:lead_rows]
    front00 = pivot_part[:, own_w:] + jnp.diag(pivot_diag)
    lead = jnp.tril(jnp.linalg.cholesky(front00))
    inv_t = lax.linalg.triangular_solve(
        lead, jnp.eye(lead_rows, dtype=jnp.float32), left_side=False, lower=True, transpose_a=True
    )
    cols_panel = jnp.where(col_index == 0, front00, pivot_part[:, :own_w]).T

    my_tiles = lax.dynamic_slice_in_dim(order, row_index * per_group, per_group, axis=1)
    my_root = jnp.take_along_axis(child_tiles, my_tiles, axis=1)
    my_local = (my_root * TILE // block_size) // row_count * tiles_block + my_root % tiles_block
    mine4 = mine.reshape(n_child, per_group, TILE, n_cols)
    front_loc = jnp.zeros((loc_tiles, TILE, n_cols), jnp.float32)
    for child in range(n_child):
        for slot in range(per_group):
            at = my_local[child, slot]
            here = lax.dynamic_index_in_dim(front_loc, at, 0, keepdims=True)
            front_loc = lax.dynamic_update_index_in_dim(
                front_loc, here + mine4[child, slot][None], at, 0
            )
    front_loc = front_loc.reshape(loc_rows, n_cols)

    local_rows = jnp.arange(loc_rows, dtype=jnp.int32)
    row_block = row_index + local_rows // block_size * row_count
    glob_rows = row_block * block_size + local_rows % block_size
    glob_cols = col_index * block_size + jnp.arange(block_size, dtype=jnp.int32)
    diag_own = jnp.where(glob_rows[:, None] == glob_cols[None, :], root_diag[None, :], 0.0)
    front_own = front_loc[:, :own_w] + diag_own
    front_pivot = front_loc[:, own_w:]

    below_rows = jnp.dot(front_pivot, inv_t, precision=highest)
    below_cols = jnp.dot(cols_panel, inv_t, precision=highest)
    schur = front_own - jnp.dot(below_rows, below_cols.T, precision=highest)

    in_lead = (row_block < NPAN)[:, None]
    lead_tiled = jnp.tile(lead, (loc_rows // lead_rows, 1))
    first_col = jnp.where(in_lead, lead_tiled, below_rows)
    rest = jnp.where(in_lead, 0.0, schur)
    return jnp.where(col_index < NPAN, first_col, rest)


def solution(mesh):
    placed = (P(None, "col", "row"), P(), P("col"))
    return jax.shard_map(
        shards, mesh=mesh, in_specs=placed, out_specs=P("row", "col"), check_vma=False
    )
```

```python
import jax
import jax.numpy as jnp
from jax import lax
from jax.sharding import PartitionSpec as P

TILE = 128
NPAN = 1


def pick_tiles(tiles4, index):
    return jnp.take_along_axis(tiles4, index[:, :, None, None], axis=1, mode="clip")


def shards(child_factors, child_tiles, root_diag):
    highest = lax.Precision.HIGHEST
    row_count = lax.axis_size("row")
    block_size = root_diag.shape[0]
    col_count = lax.axis_size("col")
    order_total = block_size * col_count
    loc_rows = order_total // row_count
    row_index = lax.axis_index("row")
    col_index = lax.axis_index("col")
    n_child = child_tiles.shape[0]
    tiles_child = child_tiles.shape[1]
    per_group = tiles_child // row_count
    tiles_block = block_size // TILE
    loc_tiles = loc_rows // TILE

    gathered = lax.all_gather(child_factors, "col", axis=1, tiled=True)
    k_loc = gathered.shape[2]
    tiles4 = gathered.reshape(n_child, tiles_child, TILE, k_loc)
    full_diag = lax.all_gather(root_diag, "col", axis=0, tiled=True)
    diag_edge = (full_diag[0] * 0).astype(jnp.int32)

    owner = (child_tiles * TILE // block_size) % row_count
    position = jnp.arange(tiles_child, dtype=jnp.int32)
    key = owner * tiles_child + position[None, :]
    rank = jnp.sum(key[:, None, :] < key[:, :, None], axis=2).astype(jnp.int32)
    order = jnp.sum(
        jnp.where(rank[:, :, None] == position[None, None, :], position[None, :, None], 0),
        axis=1,
    ).astype(jnp.int32)

    own_tiles = col_index * tiles_block + jnp.arange(tiles_block, dtype=jnp.int32)
    pivot_tiles = jnp.arange(NPAN * tiles_block, dtype=jnp.int32)
    wanted = jnp.concatenate([own_tiles, pivot_tiles])
    match = child_tiles[:, :, None] == wanted[None, None, :]
    where_at = jnp.sum(jnp.where(match, position[None, :, None], 0), axis=1).astype(jnp.int32)
    where_at = where_at + diag_edge
    present = jnp.any(match, axis=1)
    col_rows = jnp.stack(
        [
            jnp.stack(
                [
                    lax.dynamic_index_in_dim(tiles4[child], where_at[child, slot], 0, keepdims=False)
                    for slot in range(where_at.shape[1])
                ]
            )
            for child in range(n_child)
        ]
    )
    col_rows = jnp.where(present[:, :, None, None], col_rows, jnp.zeros_like(col_rows))
    n_cols = wanted.shape[0] * TILE
    col_rows = col_rows.reshape(n_child, n_cols, k_loc)
    pivot_rows = col_rows[:, tiles_block * TILE :]

    extra = jnp.einsum(
        "cnk,cmk->nm", pivot_rows, col_rows, preferred_element_type=jnp.float32
    )
    pivot_part = extra
    for shift in range(1, row_count):
        pairs = [(i, (i + shift) % row_count) for i in range(row_count)]
        pivot_part = pivot_part + lax.ppermute(extra, "row", pairs)
    main_rows = col_rows + (extra[:1, :1] * 0).astype(col_rows.dtype)[None]
    main = jnp.einsum(
        "cutk,cmk->cumt", tiles4, main_rows, preferred_element_type=jnp.float32
    )
    main = main.reshape(n_child * tiles_child, n_cols, TILE)
    child_base = (jnp.arange(n_child, dtype=jnp.int32) * tiles_child)[:, None]
    flat_order = (order + child_base).reshape(n_child, row_count, per_group)
    flat_order = jnp.transpose(flat_order, (1, 0, 2)).reshape(-1)
    main = jnp.take(main, flat_order, axis=0, mode="clip")
    mine = lax.psum_scatter(
        main.reshape(row_count * n_child * per_group * n_cols, TILE),
        "row",
        scatter_dimension=0,
        tiled=True,
    ).reshape(n_child, per_group, n_cols, TILE)
    mine = lax.optimization_barrier(jnp.transpose(mine, (0, 1, 3, 2)))

    own_w = tiles_block * TILE
    lead_rows = NPAN * block_size
    pivot_diag = full_diag[:lead_rows]
    front00 = pivot_part[:, own_w:] + jnp.diag(pivot_diag)
    lead = jnp.tril(jnp.linalg.cholesky(front00))
    inv_t = lax.linalg.triangular_solve(
        lead, jnp.eye(lead_rows, dtype=jnp.float32), left_side=False, lower=True, transpose_a=True
    )
    cols_panel = jnp.where(col_index == 0, front00, pivot_part[:, :own_w]).T

    my_tiles = lax.dynamic_slice_in_dim(order, row_index * per_group, per_group, axis=1)
    my_root = jnp.take_along_axis(child_tiles, my_tiles, axis=1)
    my_local = (my_root * TILE // block_size) // row_count * tiles_block + my_root % tiles_block
    mine4 = mine
    front_loc = jnp.zeros((loc_tiles, TILE, n_cols), jnp.float32)
    for child in range(n_child):
        for slot in range(per_group):
            at = my_local[child, slot]
            here = lax.dynamic_index_in_dim(front_loc, at, 0, keepdims=True)
            front_loc = lax.dynamic_update_index_in_dim(
                front_loc, here + mine4[child, slot][None], at, 0
            )
    front_loc = front_loc.reshape(loc_rows, n_cols)

    local_rows = jnp.arange(loc_rows, dtype=jnp.int32)
    row_block = row_index + local_rows // block_size * row_count
    glob_rows = row_block * block_size + local_rows % block_size
    glob_cols = col_index * block_size + jnp.arange(block_size, dtype=jnp.int32)
    diag_own = jnp.where(glob_rows[:, None] == glob_cols[None, :], root_diag[None, :], 0.0)
    front_own = front_loc[:, :own_w] + diag_own
    front_pivot = front_loc[:, own_w:]

    below_rows = jnp.dot(front_pivot, inv_t, precision=highest)
    below_cols = jnp.dot(cols_panel, inv_t, precision=highest)
    schur = front_own - jnp.dot(below_rows, below_cols.T, precision=highest)

    in_lead = (row_block < NPAN)[:, None]
    lead_tiled = jnp.tile(lead, (loc_rows // lead_rows, 1))
    first_col = jnp.where(in_lead, lead_tiled, below_rows)
    rest = jnp.where(in_lead, 0.0, schur)
    return jnp.where(col_index < NPAN, first_col, rest)


def solution(mesh):
    placed = (P(None, "col", "row"), P(), P("col"))
    return jax.shard_map(
        shards, mesh=mesh, in_specs=placed, out_specs=P("row", "col"), check_vma=False
    )
```

```python
import jax
import jax.numpy as jnp
from jax import lax
from jax.sharding import PartitionSpec as P

TILE = 128
NPAN = 1


def pick_tiles(tiles4, index):
    return jnp.take_along_axis(tiles4, index[:, :, None, None], axis=1, mode="clip")


def shards(child_factors, child_tiles, root_diag):
    highest = lax.Precision.HIGHEST
    row_count = lax.axis_size("row")
    block_size = root_diag.shape[0]
    col_count = lax.axis_size("col")
    order_total = block_size * col_count
    loc_rows = order_total // row_count
    row_index = lax.axis_index("row")
    col_index = lax.axis_index("col")
    n_child = child_tiles.shape[0]
    tiles_child = child_tiles.shape[1]
    per_group = tiles_child // row_count
    tiles_block = block_size // TILE
    loc_tiles = loc_rows // TILE

    gathered = lax.all_gather(child_factors, "col", axis=1, tiled=True)
    k_loc = gathered.shape[2]
    tiles4 = gathered.reshape(n_child, tiles_child, TILE, k_loc)
    full_diag = lax.all_gather(root_diag, "col", axis=0, tiled=True)
    diag_edge = (full_diag[0] * 0).astype(jnp.int32)

    owner = (child_tiles * TILE // block_size) % row_count
    position = jnp.arange(tiles_child, dtype=jnp.int32)
    key = owner * tiles_child + position[None, :]
    rank = jnp.sum(key[:, None, :] < key[:, :, None], axis=2).astype(jnp.int32)
    order = jnp.sum(
        jnp.where(rank[:, :, None] == position[None, None, :], position[None, :, None], 0),
        axis=1,
    ).astype(jnp.int32)

    own_tiles = col_index * tiles_block + jnp.arange(tiles_block, dtype=jnp.int32)
    pivot_tiles = jnp.arange(NPAN * tiles_block, dtype=jnp.int32)
    wanted = jnp.concatenate([own_tiles, pivot_tiles])
    match = child_tiles[:, :, None] == wanted[None, None, :]
    where_at = jnp.sum(jnp.where(match, position[None, :, None], 0), axis=1).astype(jnp.int32)
    where_at = where_at + diag_edge
    present = jnp.any(match, axis=1)
    col_rows = jnp.stack(
        [
            jnp.stack(
                [
                    lax.dynamic_slice(
                        tiles4, (child, where_at[child, slot], 0, 0), (1, 1, TILE, k_loc)
                    )[0, 0]
                    for slot in range(where_at.shape[1])
                ]
            )
            for child in range(n_child)
        ]
    )
    col_rows = jnp.where(present[:, :, None, None], col_rows, jnp.zeros_like(col_rows))
    n_cols = wanted.shape[0] * TILE
    col_rows = col_rows.reshape(n_child, n_cols, k_loc)
    pivot_rows = col_rows[:, tiles_block * TILE :]

    extra = jnp.einsum(
        "cnk,cmk->nm", pivot_rows, col_rows, preferred_element_type=jnp.float32
    )
    pivot_part = extra
    for shift in range(1, row_count):
        pairs = [(i, (i + shift) % row_count) for i in range(row_count)]
        pivot_part = pivot_part + lax.ppermute(extra, "row", pairs)
    main_rows = col_rows + (extra[:1, :1] * 0).astype(col_rows.dtype)[None]
    main = jnp.einsum(
        "cutk,cmk->cutm", tiles4, main_rows, preferred_element_type=jnp.float32
    )
    main = main.reshape(n_child * tiles_child, TILE, n_cols)
    child_base = (jnp.arange(n_child, dtype=jnp.int32) * tiles_child)[:, None]
    flat_order = (order + child_base).reshape(n_child, row_count, per_group)
    flat_order = jnp.transpose(flat_order, (1, 0, 2)).reshape(-1)
    flat_order = flat_order + (pivot_part[0, 0] * 0).astype(jnp.int32)
    main = jnp.take(main, flat_order, axis=0, mode="clip")
    mine = lax.psum_scatter(
        main.reshape(row_count * n_child * per_group * TILE, n_cols),
        "row",
        scatter_dimension=0,
        tiled=True,
    ).reshape(n_child, per_group * TILE, n_cols)

    own_w = tiles_block * TILE
    lead_rows = NPAN * block_size
    pivot_diag = full_diag[:lead_rows]
    front00 = pivot_part[:, own_w:] + jnp.diag(pivot_diag)
    lead = jnp.tril(jnp.linalg.cholesky(front00))
    inv_t = lax.linalg.triangular_solve(
        lead, jnp.eye(lead_rows, dtype=jnp.float32), left_side=False, lower=True, transpose_a=True
    )
    cols_panel = jnp.where(col_index == 0, front00, pivot_part[:, :own_w]).T

    my_tiles = lax.dynamic_slice_in_dim(order, row_index * per_group, per_group, axis=1)
    my_root = jnp.take_along_axis(child_tiles, my_tiles, axis=1)
    my_local = (my_root * TILE // block_size) // row_count * tiles_block + my_root % tiles_block
    mine4 = mine.reshape(n_child, per_group, TILE, n_cols)
    front_loc = jnp.zeros((loc_tiles, TILE, n_cols), jnp.float32)
    for child in range(n_child):
        for slot in range(per_group):
            at = my_local[child, slot]
            here = lax.dynamic_index_in_dim(front_loc, at, 0, keepdims=True)
            front_loc = lax.dynamic_update_index_in_dim(
                front_loc, here + mine4[child, slot][None], at, 0
            )
    front_loc = front_loc.reshape(loc_rows, n_cols)

    local_rows = jnp.arange(loc_rows, dtype=jnp.int32)
    row_block = row_index + local_rows // block_size * row_count
    glob_rows = row_block * block_size + local_rows % block_size
    glob_cols = col_index * block_size + jnp.arange(block_size, dtype=jnp.int32)
    diag_own = jnp.where(glob_rows[:, None] == glob_cols[None, :], root_diag[None, :], 0.0)
    front_own = front_loc[:, :own_w] + diag_own
    front_pivot = front_loc[:, own_w:]

    below_rows = jnp.dot(front_pivot, inv_t, precision=highest)
    below_cols = jnp.dot(cols_panel, inv_t, precision=highest)
    schur = front_own - jnp.dot(below_rows, below_cols.T, precision=highest)

    in_lead = (row_block < NPAN)[:, None]
    lead_tiled = jnp.tile(lead, (loc_rows // lead_rows, 1))
    first_col = jnp.where(in_lead, lead_tiled, below_rows)
    rest = jnp.where(in_lead, 0.0, schur)
    return jnp.where(col_index < NPAN, first_col, rest)


def solution(mesh):
    placed = (P(None, "col", "row"), P(), P("col"))
    return jax.shard_map(
        shards, mesh=mesh, in_specs=placed, out_specs=P("row", "col"), check_vma=False
    )
```

```python
import jax
import jax.numpy as jnp
from jax import lax
from jax.sharding import PartitionSpec as P

TILE = 128
NPAN = 1


def pick_tiles(tiles4, index):
    return jnp.take_along_axis(tiles4, index[:, :, None, None], axis=1, mode="clip")


def shards(child_factors, child_tiles, root_diag):
    highest = lax.Precision.HIGHEST
    row_count = lax.axis_size("row")
    block_size = root_diag.shape[0]
    col_count = lax.axis_size("col")
    order_total = block_size * col_count
    loc_rows = order_total // row_count
    row_index = lax.axis_index("row")
    col_index = lax.axis_index("col")
    n_child = child_tiles.shape[0]
    tiles_child = child_tiles.shape[1]
    per_group = tiles_child // row_count
    tiles_block = block_size // TILE
    loc_tiles = loc_rows // TILE

    gathered = lax.all_gather(child_factors, "col", axis=1, tiled=True)
    k_loc = gathered.shape[2]
    tiles4 = gathered.reshape(n_child, tiles_child, TILE, k_loc)
    full_diag = lax.all_gather(root_diag, "col", axis=0, tiled=True)
    diag_edge = (full_diag[0] * 0).astype(jnp.int32)

    owner = (child_tiles * TILE // block_size) % row_count
    position = jnp.arange(tiles_child, dtype=jnp.int32)
    key = owner * tiles_child + position[None, :]
    rank = jnp.sum(key[:, None, :] < key[:, :, None], axis=2).astype(jnp.int32)
    order = jnp.sum(
        jnp.where(rank[:, :, None] == position[None, None, :], position[None, :, None], 0),
        axis=1,
    ).astype(jnp.int32)

    own_tiles = col_index * tiles_block + jnp.arange(tiles_block, dtype=jnp.int32)
    pivot_tiles = jnp.arange(NPAN * tiles_block, dtype=jnp.int32)
    wanted = jnp.concatenate([own_tiles, pivot_tiles])
    match = child_tiles[:, :, None] == wanted[None, None, :]
    where_at = jnp.sum(jnp.where(match, position[None, :, None], 0), axis=1).astype(jnp.int32)
    my_tiles = lax.dynamic_slice_in_dim(order, row_index * per_group, per_group, axis=1)
    my_root = jnp.take_along_axis(child_tiles, my_tiles, axis=1)
    my_local = (my_root * TILE // block_size) // row_count * tiles_block + my_root % tiles_block
    n_slots = where_at.size
    all_index = jnp.concatenate([where_at.reshape(-1), my_local.reshape(-1)]) + diag_edge
    where_at = all_index[:n_slots].reshape(where_at.shape)
    my_local = all_index[n_slots:].reshape(my_local.shape)
    present = jnp.any(match, axis=1)
    col_rows = jnp.stack(
        [
            jnp.stack(
                [
                    lax.dynamic_slice(
                        tiles4, (child, where_at[child, slot], 0, 0), (1, 1, TILE, k_loc)
                    )[0, 0]
                    for slot in range(where_at.shape[1])
                ]
            )
            for child in range(n_child)
        ]
    )
    col_rows = jnp.where(present[:, :, None, None], col_rows, jnp.zeros_like(col_rows))
    n_cols = wanted.shape[0] * TILE
    col_rows = col_rows.reshape(n_child, n_cols, k_loc)
    pivot_rows = col_rows[:, tiles_block * TILE :]

    extra = jnp.einsum(
        "cnk,cmk->nm", pivot_rows, col_rows, preferred_element_type=jnp.float32
    )
    pivot_part = extra
    for shift in range(1, row_count):
        pairs = [(i, (i + shift) % row_count) for i in range(row_count)]
        pivot_part = pivot_part + lax.ppermute(extra, "row", pairs)
    main_rows = col_rows + (extra[:1, :1] * 0).astype(col_rows.dtype)[None]
    main = jnp.einsum(
        "cutk,cmk->cutm", tiles4, main_rows, preferred_element_type=jnp.float32
    )
    main = main.reshape(n_child * tiles_child, TILE, n_cols)
    child_base = (jnp.arange(n_child, dtype=jnp.int32) * tiles_child)[:, None]
    flat_order = (order + child_base).reshape(n_child, row_count, per_group)
    flat_order = jnp.transpose(flat_order, (1, 0, 2)).reshape(-1)
    flat_order = flat_order + (pivot_part[0, 0] * 0).astype(jnp.int32)
    main = jnp.take(main, flat_order, axis=0, mode="clip")
    mine = lax.psum_scatter(
        main.reshape(row_count * n_child * per_group * TILE, n_cols),
        "row",
        scatter_dimension=0,
        tiled=True,
    ).reshape(n_child, per_group * TILE, n_cols)

    own_w = tiles_block * TILE
    lead_rows = NPAN * block_size
    pivot_diag = full_diag[:lead_rows]
    front00 = pivot_part[:, own_w:] + jnp.diag(pivot_diag)
    lead = jnp.tril(jnp.linalg.cholesky(front00))
    inv_t = lax.linalg.triangular_solve(
        lead, jnp.eye(lead_rows, dtype=jnp.float32), left_side=False, lower=True, transpose_a=True
    )
    cols_panel = jnp.where(col_index == 0, front00, pivot_part[:, :own_w]).T

    mine4 = mine.reshape(n_child, per_group, TILE, n_cols)
    front_loc = jnp.zeros((loc_tiles, TILE, n_cols), jnp.float32)
    for child in range(n_child):
        for slot in range(per_group):
            at = my_local[child, slot]
            here = lax.dynamic_index_in_dim(front_loc, at, 0, keepdims=True)
            front_loc = lax.dynamic_update_index_in_dim(
                front_loc, here + mine4[child, slot][None], at, 0
            )
    front_loc = front_loc.reshape(loc_rows, n_cols)

    local_rows = jnp.arange(loc_rows, dtype=jnp.int32)
    row_block = row_index + local_rows // block_size * row_count
    glob_rows = row_block * block_size + local_rows % block_size
    glob_cols = col_index * block_size + jnp.arange(block_size, dtype=jnp.int32)
    diag_own = jnp.where(glob_rows[:, None] == glob_cols[None, :], root_diag[None, :], 0.0)
    front_own = front_loc[:, :own_w] + diag_own
    front_pivot = front_loc[:, own_w:]

    below_rows = jnp.dot(front_pivot, inv_t, precision=highest)
    below_cols = jnp.dot(cols_panel, inv_t, precision=highest)
    schur = front_own - jnp.dot(below_rows, below_cols.T, precision=highest)

    in_lead = (row_block < NPAN)[:, None]
    lead_tiled = jnp.tile(lead, (loc_rows // lead_rows, 1))
    first_col = jnp.where(in_lead, lead_tiled, below_rows)
    rest = jnp.where(in_lead, 0.0, schur)
    return jnp.where(col_index < NPAN, first_col, rest)


def solution(mesh):
    placed = (P(None, "col", "row"), P(), P("col"))
    return jax.shard_map(
        shards, mesh=mesh, in_specs=placed, out_specs=P("row", "col"), check_vma=False
    )
```

```python
import jax
import jax.numpy as jnp
from jax import lax
from jax.sharding import PartitionSpec as P

TILE = 128
NPAN = 1


def pick_tiles(tiles4, index):
    return jnp.take_along_axis(tiles4, index[:, :, None, None], axis=1, mode="clip")


def shards(child_factors, child_tiles, root_diag):
    highest = lax.Precision.HIGHEST
    row_count = lax.axis_size("row")
    block_size = root_diag.shape[0]
    col_count = lax.axis_size("col")
    order_total = block_size * col_count
    loc_rows = order_total // row_count
    row_index = lax.axis_index("row")
    col_index = lax.axis_index("col")
    n_child = child_tiles.shape[0]
    tiles_child = child_tiles.shape[1]
    per_group = tiles_child // row_count
    tiles_block = block_size // TILE
    loc_tiles = loc_rows // TILE

    gathered = lax.all_gather(child_factors, "col", axis=1, tiled=True)
    k_loc = gathered.shape[2]
    tiles4 = gathered.reshape(n_child, tiles_child, TILE, k_loc)
    full_diag = lax.all_gather(root_diag, "col", axis=0, tiled=True)
    diag_edge = (full_diag[0] * 0).astype(jnp.int32)

    owner = (child_tiles * TILE // block_size) % row_count
    position = jnp.arange(tiles_child, dtype=jnp.int32)
    key = owner * tiles_child + position[None, :]
    rank = jnp.sum(key[:, None, :] < key[:, :, None], axis=2).astype(jnp.int32)
    order = jnp.sum(
        jnp.where(rank[:, :, None] == position[None, None, :], position[None, :, None], 0),
        axis=1,
    ).astype(jnp.int32)

    own_tiles = col_index * tiles_block + jnp.arange(tiles_block, dtype=jnp.int32)
    pivot_tiles = jnp.arange(NPAN * tiles_block, dtype=jnp.int32)
    wanted = jnp.concatenate([own_tiles, pivot_tiles])
    match = child_tiles[:, :, None] == wanted[None, None, :]
    where_at = jnp.sum(jnp.where(match, position[None, :, None], 0), axis=1).astype(jnp.int32)
    where_at = where_at + diag_edge
    present = jnp.any(match, axis=1)
    col_rows = jnp.stack(
        [
            jnp.stack(
                [
                    lax.dynamic_slice(
                        tiles4, (child, where_at[child, slot], 0, 0), (1, 1, TILE, k_loc)
                    )[0, 0]
                    for slot in range(where_at.shape[1])
                ]
            )
            for child in range(n_child)
        ]
    )
    col_rows = jnp.where(present[:, :, None, None], col_rows, jnp.zeros_like(col_rows))
    n_cols = wanted.shape[0] * TILE
    col_rows = col_rows.reshape(n_child, n_cols, k_loc)
    pivot_rows = col_rows[:, tiles_block * TILE :]

    extra = jnp.einsum(
        "cnk,cmk->nm", pivot_rows, col_rows, preferred_element_type=jnp.float32
    )
    pivot_part = extra
    for shift in range(1, row_count):
        pairs = [(i, (i + shift) % row_count) for i in range(row_count)]
        pivot_part = pivot_part + lax.ppermute(extra, "row", pairs)
    main_rows = col_rows + (extra[:1, :1] * 0).astype(col_rows.dtype)[None]
    main = jnp.einsum(
        "cutk,cmk->cutm", tiles4, main_rows, preferred_element_type=jnp.float32
    )
    main = main.reshape(n_child * tiles_child, TILE, n_cols)
    child_base = (jnp.arange(n_child, dtype=jnp.int32) * tiles_child)[:, None]
    flat_order = (order + child_base).reshape(n_child, row_count, per_group)
    flat_order = jnp.transpose(flat_order, (1, 0, 2)).reshape(-1)
    flat_order = flat_order + (pivot_part[0, 0] * 0).astype(jnp.int32)
    main = jnp.take(main, flat_order, axis=0, mode="clip")
    mine = lax.psum_scatter(
        main.reshape(row_count * n_child * per_group * TILE, n_cols),
        "row",
        scatter_dimension=0,
        tiled=True,
    ).reshape(n_child, per_group * TILE, n_cols)

    own_w = tiles_block * TILE
    lead_rows = NPAN * block_size
    pivot_diag = full_diag[:lead_rows]
    front00 = pivot_part[:, own_w:] + jnp.diag(pivot_diag)
    lead = jnp.tril(jnp.linalg.cholesky(front00))
    inv_t = lax.linalg.triangular_solve(
        lead, jnp.eye(lead_rows, dtype=jnp.float32), left_side=False, lower=True, transpose_a=True
    )
    cols_panel = jnp.where(col_index == 0, front00, pivot_part[:, :own_w]).T

    my_tiles = lax.dynamic_slice_in_dim(order, row_index * per_group, per_group, axis=1)
    my_root = jnp.take_along_axis(child_tiles, my_tiles, axis=1)
    my_local = (my_root * TILE // block_size) // row_count * tiles_block + my_root % tiles_block
    mine4 = mine.reshape(n_child, per_group, TILE, n_cols)
    onto = (my_local[:, None, :] == jnp.arange(loc_tiles, dtype=jnp.int32)[None, :, None])
    front_loc = jnp.einsum(
        "cls,cstm->ltm", onto.astype(jnp.float32), mine4, precision=highest
    )
    front_loc = front_loc.reshape(loc_rows, n_cols)

    local_rows = jnp.arange(loc_rows, dtype=jnp.int32)
    row_block = row_index + local_rows // block_size * row_count
    glob_rows = row_block * block_size + local_rows % block_size
    glob_cols = col_index * block_size + jnp.arange(block_size, dtype=jnp.int32)
    diag_own = jnp.where(glob_rows[:, None] == glob_cols[None, :], root_diag[None, :], 0.0)
    front_own = front_loc[:, :own_w] + diag_own
    front_pivot = front_loc[:, own_w:]

    below_rows = jnp.dot(front_pivot, inv_t, precision=highest)
    below_cols = jnp.dot(cols_panel, inv_t, precision=highest)
    schur = front_own - jnp.dot(below_rows, below_cols.T, precision=highest)

    in_lead = (row_block < NPAN)[:, None]
    lead_tiled = jnp.tile(lead, (loc_rows // lead_rows, 1))
    first_col = jnp.where(in_lead, lead_tiled, below_rows)
    rest = jnp.where(in_lead, 0.0, schur)
    return jnp.where(col_index < NPAN, first_col, rest)


def solution(mesh):
    placed = (P(None, "col", "row"), P(), P("col"))
    return jax.shard_map(
        shards, mesh=mesh, in_specs=placed, out_specs=P("row", "col"), check_vma=False
    )
```

```python
import jax
import jax.numpy as jnp
from jax import lax
from jax.sharding import PartitionSpec as P

TILE = 128
NPAN = 1


def pick_tiles(tiles4, index):
    return jnp.take_along_axis(tiles4, index[:, :, None, None], axis=1, mode="clip")


def shards(child_factors, child_tiles, root_diag):
    highest = lax.Precision.HIGHEST
    row_count = lax.axis_size("row")
    block_size = root_diag.shape[0]
    col_count = lax.axis_size("col")
    order_total = block_size * col_count
    loc_rows = order_total // row_count
    row_index = lax.axis_index("row")
    col_index = lax.axis_index("col")
    n_child = child_tiles.shape[0]
    tiles_child = child_tiles.shape[1]
    per_group = tiles_child // row_count
    tiles_block = block_size // TILE
    loc_tiles = loc_rows // TILE

    gathered = lax.all_gather(child_factors, "col", axis=1, tiled=True)
    k_loc = gathered.shape[2]
    tiles4 = gathered.reshape(n_child, tiles_child, TILE, k_loc)
    full_diag = lax.all_gather(root_diag, "col", axis=0, tiled=True)
    diag_edge = (full_diag[0] * 0).astype(jnp.int32)

    owner = (child_tiles * TILE // block_size) % row_count
    position = jnp.arange(tiles_child, dtype=jnp.int32)
    key = owner * tiles_child + position[None, :]
    rank = jnp.sum(key[:, None, :] < key[:, :, None], axis=2).astype(jnp.int32)
    order = jnp.sum(
        jnp.where(rank[:, :, None] == position[None, None, :], position[None, :, None], 0),
        axis=1,
    ).astype(jnp.int32)

    own_tiles = col_index * tiles_block + jnp.arange(tiles_block, dtype=jnp.int32)
    pivot_tiles = jnp.arange(NPAN * tiles_block, dtype=jnp.int32)
    wanted = jnp.concatenate([own_tiles, pivot_tiles])
    match = child_tiles[:, :, None] == wanted[None, None, :]
    where_at = jnp.sum(jnp.where(match, position[None, :, None], 0), axis=1).astype(jnp.int32)
    where_at = where_at + diag_edge
    present = jnp.any(match, axis=1)
    col_rows = jnp.stack(
        [
            jnp.stack(
                [
                    lax.dynamic_slice(
                        tiles4, (child, where_at[child, slot], 0, 0), (1, 1, TILE, k_loc)
                    )[0, 0]
                    for slot in range(where_at.shape[1])
                ]
            )
            for child in range(n_child)
        ]
    )
    col_rows = jnp.where(present[:, :, None, None], col_rows, jnp.zeros_like(col_rows))
    n_cols = wanted.shape[0] * TILE
    col_rows = col_rows.reshape(n_child, n_cols, k_loc)
    pivot_rows = col_rows[:, tiles_block * TILE :]

    extra = jnp.einsum(
        "cnk,cmk->nm", pivot_rows, col_rows, preferred_element_type=jnp.float32
    )
    pivot_part = extra
    step = 1
    while step < row_count:
        pairs = [(i, i ^ step) for i in range(row_count)]
        pivot_part = pivot_part + lax.ppermute(pivot_part, "row", pairs)
        step *= 2
    main_rows = col_rows + (extra[:1, :1] * 0).astype(col_rows.dtype)[None]
    main = jnp.einsum(
        "cutk,cmk->cutm", tiles4, main_rows, preferred_element_type=jnp.float32
    )
    main = main.reshape(n_child * tiles_child, TILE, n_cols)
    child_base = (jnp.arange(n_child, dtype=jnp.int32) * tiles_child)[:, None]
    flat_order = (order + child_base).reshape(n_child, row_count, per_group)
    flat_order = jnp.transpose(flat_order, (1, 0, 2)).reshape(-1)
    flat_order = flat_order + (pivot_part[0, 0] * 0).astype(jnp.int32)
    main = jnp.take(main, flat_order, axis=0, mode="clip")
    mine = lax.psum_scatter(
        main.reshape(row_count * n_child * per_group * TILE, n_cols),
        "row",
        scatter_dimension=0,
        tiled=True,
    ).reshape(n_child, per_group * TILE, n_cols)

    own_w = tiles_block * TILE
    lead_rows = NPAN * block_size
    pivot_diag = full_diag[:lead_rows]
    front00 = pivot_part[:, own_w:] + jnp.diag(pivot_diag)
    lead = jnp.tril(jnp.linalg.cholesky(front00))
    inv_t = lax.linalg.triangular_solve(
        lead, jnp.eye(lead_rows, dtype=jnp.float32), left_side=False, lower=True, transpose_a=True
    )
    cols_panel = jnp.where(col_index == 0, front00, pivot_part[:, :own_w]).T

    my_tiles = lax.dynamic_slice_in_dim(order, row_index * per_group, per_group, axis=1)
    my_root = jnp.take_along_axis(child_tiles, my_tiles, axis=1)
    my_local = (my_root * TILE // block_size) // row_count * tiles_block + my_root % tiles_block
    mine4 = mine.reshape(n_child, per_group, TILE, n_cols)
    front_loc = jnp.zeros((loc_tiles, TILE, n_cols), jnp.float32)
    for child in range(n_child):
        for slot in range(per_group):
            at = my_local[child, slot]
            here = lax.dynamic_index_in_dim(front_loc, at, 0, keepdims=True)
            front_loc = lax.dynamic_update_index_in_dim(
                front_loc, here + mine4[child, slot][None], at, 0
            )
    front_loc = front_loc.reshape(loc_rows, n_cols)

    local_rows = jnp.arange(loc_rows, dtype=jnp.int32)
    row_block = row_index + local_rows // block_size * row_count
    glob_rows = row_block * block_size + local_rows % block_size
    glob_cols = col_index * block_size + jnp.arange(block_size, dtype=jnp.int32)
    diag_own = jnp.where(glob_rows[:, None] == glob_cols[None, :], root_diag[None, :], 0.0)
    front_own = front_loc[:, :own_w] + diag_own
    front_pivot = front_loc[:, own_w:]

    below_rows = jnp.dot(front_pivot, inv_t, precision=highest)
    below_cols = jnp.dot(cols_panel, inv_t, precision=highest)
    schur = front_own - jnp.dot(below_rows, below_cols.T, precision=highest)

    in_lead = (row_block < NPAN)[:, None]
    lead_tiled = jnp.tile(lead, (loc_rows // lead_rows, 1))
    first_col = jnp.where(in_lead, lead_tiled, below_rows)
    rest = jnp.where(in_lead, 0.0, schur)
    return jnp.where(col_index < NPAN, first_col, rest)


def solution(mesh):
    placed = (P(None, "col", "row"), P(), P("col"))
    return jax.shard_map(
        shards, mesh=mesh, in_specs=placed, out_specs=P("row", "col"), check_vma=False
    )
```

```python
import jax
import jax.numpy as jnp
from jax import lax
from jax.sharding import PartitionSpec as P

TILE = 128
NPAN = 1


def pick_tiles(tiles4, index):
    return jnp.take_along_axis(tiles4, index[:, :, None, None], axis=1, mode="clip")


def shards(child_factors, child_tiles, root_diag):
    highest = lax.Precision.HIGHEST
    row_count = lax.axis_size("row")
    block_size = root_diag.shape[0]
    col_count = lax.axis_size("col")
    order_total = block_size * col_count
    loc_rows = order_total // row_count
    row_index = lax.axis_index("row")
    col_index = lax.axis_index("col")
    n_child = child_tiles.shape[0]
    tiles_child = child_tiles.shape[1]
    per_group = tiles_child // row_count
    tiles_block = block_size // TILE
    loc_tiles = loc_rows // TILE

    gathered = lax.all_gather(child_factors, "col", axis=1, tiled=True)
    k_loc = gathered.shape[2]
    tiles4 = gathered.reshape(n_child, tiles_child, TILE, k_loc)
    full_diag = lax.all_gather(root_diag, "col", axis=0, tiled=True)
    diag_edge = (full_diag[0] * 0).astype(jnp.int32)

    owner = (child_tiles * TILE // block_size) % row_count
    position = jnp.arange(tiles_child, dtype=jnp.int32)
    key = owner * tiles_child + position[None, :]
    rank = jnp.sum(key[:, None, :] < key[:, :, None], axis=2).astype(jnp.int32)
    order = jnp.sum(
        jnp.where(rank[:, :, None] == position[None, None, :], position[None, :, None], 0),
        axis=1,
    ).astype(jnp.int32)

    own_tiles = col_index * tiles_block + jnp.arange(tiles_block, dtype=jnp.int32)
    pivot_tiles = jnp.arange(NPAN * tiles_block, dtype=jnp.int32)
    wanted = jnp.concatenate([own_tiles, pivot_tiles])
    match = child_tiles[:, :, None] == wanted[None, None, :]
    where_at = jnp.sum(jnp.where(match, position[None, :, None], 0), axis=1).astype(jnp.int32)
    my_tiles = lax.dynamic_slice_in_dim(order, row_index * per_group, per_group, axis=1)
    my_root = jnp.take_along_axis(child_tiles, my_tiles, axis=1)
    my_local = (my_root * TILE // block_size) // row_count * tiles_block + my_root % tiles_block
    tile_ids = jnp.arange(loc_tiles, dtype=jnp.int32)
    seen = sum(
        lax.dynamic_index_in_dim(tile_ids, my_local[child, slot], 0, keepdims=False)
        for child in range(n_child)
        for slot in range(per_group)
    )
    where_at = where_at + diag_edge * (1 + seen)
    present = jnp.any(match, axis=1)
    col_rows = jnp.stack(
        [
            jnp.stack(
                [
                    lax.dynamic_slice(
                        tiles4, (child, where_at[child, slot], 0, 0), (1, 1, TILE, k_loc)
                    )[0, 0]
                    for slot in range(where_at.shape[1])
                ]
            )
            for child in range(n_child)
        ]
    )
    col_rows = jnp.where(present[:, :, None, None], col_rows, jnp.zeros_like(col_rows))
    n_cols = wanted.shape[0] * TILE
    col_rows = col_rows.reshape(n_child, n_cols, k_loc)
    pivot_rows = col_rows[:, tiles_block * TILE :]

    extra = jnp.einsum(
        "cnk,cmk->nm", pivot_rows, col_rows, preferred_element_type=jnp.float32
    )
    pivot_part = extra
    for shift in range(1, row_count):
        pairs = [(i, (i + shift) % row_count) for i in range(row_count)]
        pivot_part = pivot_part + lax.ppermute(extra, "row", pairs)
    main_rows = col_rows + (extra[:1, :1] * 0).astype(col_rows.dtype)[None]
    main = jnp.einsum(
        "cutk,cmk->cutm", tiles4, main_rows, preferred_element_type=jnp.float32
    )
    main = main.reshape(n_child * tiles_child, TILE, n_cols)
    child_base = (jnp.arange(n_child, dtype=jnp.int32) * tiles_child)[:, None]
    flat_order = (order + child_base).reshape(n_child, row_count, per_group)
    flat_order = jnp.transpose(flat_order, (1, 0, 2)).reshape(-1)
    flat_order = flat_order + (pivot_part[0, 0] * 0).astype(jnp.int32)
    main = jnp.take(main, flat_order, axis=0, mode="clip")
    mine = lax.psum_scatter(
        main.reshape(row_count * n_child * per_group * TILE, n_cols),
        "row",
        scatter_dimension=0,
        tiled=True,
    ).reshape(n_child, per_group * TILE, n_cols)

    own_w = tiles_block * TILE
    lead_rows = NPAN * block_size
    pivot_diag = full_diag[:lead_rows]
    front00 = pivot_part[:, own_w:] + jnp.diag(pivot_diag)
    lead = jnp.tril(jnp.linalg.cholesky(front00))
    inv_t = lax.linalg.triangular_solve(
        lead, jnp.eye(lead_rows, dtype=jnp.float32), left_side=False, lower=True, transpose_a=True
    )
    cols_panel = jnp.where(col_index == 0, front00, pivot_part[:, :own_w]).T

    mine4 = mine.reshape(n_child, per_group, TILE, n_cols)
    front_loc = jnp.zeros((loc_tiles, TILE, n_cols), jnp.float32)
    for child in range(n_child):
        for slot in range(per_group):
            at = my_local[child, slot]
            here = lax.dynamic_index_in_dim(front_loc, at, 0, keepdims=True)
            front_loc = lax.dynamic_update_index_in_dim(
                front_loc, here + mine4[child, slot][None], at, 0
            )
    front_loc = front_loc.reshape(loc_rows, n_cols)

    local_rows = jnp.arange(loc_rows, dtype=jnp.int32)
    row_block = row_index + local_rows // block_size * row_count
    glob_rows = row_block * block_size + local_rows % block_size
    glob_cols = col_index * block_size + jnp.arange(block_size, dtype=jnp.int32)
    diag_own = jnp.where(glob_rows[:, None] == glob_cols[None, :], root_diag[None, :], 0.0)
    front_own = front_loc[:, :own_w] + diag_own
    front_pivot = front_loc[:, own_w:]

    below_rows = jnp.dot(front_pivot, inv_t, precision=highest)
    below_cols = jnp.dot(cols_panel, inv_t, precision=highest)
    schur = front_own - jnp.dot(below_rows, below_cols.T, precision=highest)

    in_lead = (row_block < NPAN)[:, None]
    lead_tiled = jnp.tile(lead, (loc_rows // lead_rows, 1))
    first_col = jnp.where(in_lead, lead_tiled, below_rows)
    rest = jnp.where(in_lead, 0.0, schur)
    return jnp.where(col_index < NPAN, first_col, rest)


def solution(mesh):
    placed = (P(None, "col", "row"), P(), P("col"))
    return jax.shard_map(
        shards, mesh=mesh, in_specs=placed, out_specs=P("row", "col"), check_vma=False
    )
```

```python
import jax
import jax.numpy as jnp
from jax import lax
from jax.sharding import PartitionSpec as P

TILE = 128
NPAN = 1


def pick_tiles(tiles4, index):
    return jnp.take_along_axis(tiles4, index[:, :, None, None], axis=1, mode="clip")


def shards(child_factors, child_tiles, root_diag):
    highest = lax.Precision.HIGHEST
    row_count = lax.axis_size("row")
    block_size = root_diag.shape[0]
    col_count = lax.axis_size("col")
    order_total = block_size * col_count
    loc_rows = order_total // row_count
    row_index = lax.axis_index("row")
    col_index = lax.axis_index("col")
    n_child = child_tiles.shape[0]
    tiles_child = child_tiles.shape[1]
    per_group = tiles_child // row_count
    tiles_block = block_size // TILE
    loc_tiles = loc_rows // TILE

    gathered = lax.all_gather(child_factors, "col", axis=1, tiled=True)
    k_loc = gathered.shape[2]
    tiles4 = gathered.reshape(n_child, tiles_child, TILE, k_loc)
    full_diag = lax.all_gather(root_diag, "col", axis=0, tiled=True)
    diag_edge = (full_diag[0] * 0).astype(jnp.int32)

    owner = (child_tiles * TILE // block_size) % row_count
    position = jnp.arange(tiles_child, dtype=jnp.int32)
    key = owner * tiles_child + position[None, :]
    rank = jnp.sum(key[:, None, :] < key[:, :, None], axis=2).astype(jnp.int32)
    order = jnp.sum(
        jnp.where(rank[:, :, None] == position[None, None, :], position[None, :, None], 0),
        axis=1,
    ).astype(jnp.int32)

    own_tiles = col_index * tiles_block + jnp.arange(tiles_block, dtype=jnp.int32)
    pivot_tiles = jnp.arange(NPAN * tiles_block, dtype=jnp.int32)
    wanted = jnp.concatenate([own_tiles, pivot_tiles])
    match = child_tiles[:, :, None] == wanted[None, None, :]
    where_at = jnp.sum(jnp.where(match, position[None, :, None], 0), axis=1).astype(jnp.int32)
    my_tiles = lax.dynamic_slice_in_dim(order, row_index * per_group, per_group, axis=1)
    my_root = jnp.take_along_axis(child_tiles, my_tiles, axis=1)
    my_local = (my_root * TILE // block_size) // row_count * tiles_block + my_root % tiles_block
    tile_ids = jnp.arange(loc_tiles, dtype=jnp.int32)
    seen = sum(
        lax.dynamic_index_in_dim(tile_ids, my_local[child, slot], 0, keepdims=False)
        for child in range(n_child)
        for slot in range(per_group)
    )
    where_at = where_at + diag_edge * (1 + seen)
    present = jnp.any(match, axis=1)
    col_rows = jnp.stack(
        [
            jnp.stack(
                [
                    lax.dynamic_slice(
                        tiles4, (child, where_at[child, slot], 0, 0), (1, 1, TILE, k_loc)
                    )[0, 0]
                    for slot in range(where_at.shape[1])
                ]
            )
            for child in range(n_child)
        ]
    )
    col_rows = jnp.where(present[:, :, None, None], col_rows, jnp.zeros_like(col_rows))
    n_cols = wanted.shape[0] * TILE
    col_rows = col_rows.reshape(n_child, n_cols, k_loc)
    pivot_rows = col_rows[:, tiles_block * TILE :]

    extra = jnp.einsum(
        "cnk,cmk->nm", pivot_rows, col_rows, preferred_element_type=jnp.float32
    )
    pivot_part = extra
    arrived = 0.0
    for shift in range(1, row_count):
        pairs = [(i, (i + shift) % row_count) for i in range(row_count)]
        moved = lax.ppermute(extra, "row", pairs)
        arrived = arrived + moved[0, 0]
        pivot_part = pivot_part + moved
    main_rows = col_rows + (extra[:1, :1] * 0).astype(col_rows.dtype)[None]
    main = jnp.einsum(
        "cutk,cmk->cutm", tiles4, main_rows, preferred_element_type=jnp.float32
    )
    main = main.reshape(n_child * tiles_child, TILE, n_cols)
    child_base = (jnp.arange(n_child, dtype=jnp.int32) * tiles_child)[:, None]
    flat_order = (order + child_base).reshape(n_child, row_count, per_group)
    flat_order = jnp.transpose(flat_order, (1, 0, 2)).reshape(-1)
    flat_order = flat_order + (arrived * 0).astype(jnp.int32)
    main = jnp.take(main, flat_order, axis=0, mode="clip")
    mine = lax.psum_scatter(
        main.reshape(row_count * n_child * per_group * TILE, n_cols),
        "row",
        scatter_dimension=0,
        tiled=True,
    ).reshape(n_child, per_group * TILE, n_cols)

    own_w = tiles_block * TILE
    lead_rows = NPAN * block_size
    pivot_diag = full_diag[:lead_rows]
    front00 = pivot_part[:, own_w:] + jnp.diag(pivot_diag)
    lead = jnp.tril(jnp.linalg.cholesky(front00))
    inv_t = lax.linalg.triangular_solve(
        lead, jnp.eye(lead_rows, dtype=jnp.float32), left_side=False, lower=True, transpose_a=True
    )
    cols_panel = jnp.where(col_index == 0, front00, pivot_part[:, :own_w]).T

    mine4 = mine.reshape(n_child, per_group, TILE, n_cols)
    front_loc = jnp.zeros((loc_tiles, TILE, n_cols), jnp.float32)
    for child in range(n_child):
        for slot in range(per_group):
            at = my_local[child, slot]
            here = lax.dynamic_index_in_dim(front_loc, at, 0, keepdims=True)
            front_loc = lax.dynamic_update_index_in_dim(
                front_loc, here + mine4[child, slot][None], at, 0
            )
    front_loc = front_loc.reshape(loc_rows, n_cols)

    local_rows = jnp.arange(loc_rows, dtype=jnp.int32)
    row_block = row_index + local_rows // block_size * row_count
    glob_rows = row_block * block_size + local_rows % block_size
    glob_cols = col_index * block_size + jnp.arange(block_size, dtype=jnp.int32)
    diag_own = jnp.where(glob_rows[:, None] == glob_cols[None, :], root_diag[None, :], 0.0)
    front_own = front_loc[:, :own_w] + diag_own
    front_pivot = front_loc[:, own_w:]

    below_rows = jnp.dot(front_pivot, inv_t, precision=highest)
    below_cols = jnp.dot(cols_panel, inv_t, precision=highest)
    schur = front_own - jnp.dot(below_rows, below_cols.T, precision=highest)

    in_lead = (row_block < NPAN)[:, None]
    lead_tiled = jnp.tile(lead, (loc_rows // lead_rows, 1))
    first_col = jnp.where(in_lead, lead_tiled, below_rows)
    rest = jnp.where(in_lead, 0.0, schur)
    return jnp.where(col_index < NPAN, first_col, rest)


def solution(mesh):
    placed = (P(None, "col", "row"), P(), P("col"))
    return jax.shard_map(
        shards, mesh=mesh, in_specs=placed, out_specs=P("row", "col"), check_vma=False
    )
```
